32 devices in a mesh: group: 2 (over x), gx: 16 (over z, y, core).
Axes of the slice: x: 2, y: 2, z: 4, core: 2. Of those that a mesh axis runs over, the one named last changes fastest.
Arguments:
- fields: float32 [128, 256, 256], P(('group', 'gx')), parts along dimension 0, may hold values from -6 to 6
- courant: float32 [128, 16384], P(('group', 'gx')), parts along dimension 0, may hold values from -0.8 to 0.8
- switches: int32 [2, 128, 16384], P(None, ('group', 'gx')), parts along dimension 1, may hold values 0 or 1
- strip_table: int32 [512], P('group'), parts along dimension 0, may hold values from 0 to 15, never falling along the last dimension, each value on 1 to 32 neighbouring positions
- weight_in: bfloat16 [2304, 256], replicated, may hold values from -0.125 to 0.125
- bias_in: float32 [256], replicated, may hold values from -3 to 3
- weight_mid: bfloat16 [16, 256, 256], P('gx'), may hold values from -0.375 to 0.375
- bias_mid: float32 [16, 256], P('gx'), may hold values from -3 to 3
- weight_out: bfloat16 [16, 256, 256], P('gx'), may hold values from -0.375 to 0.375
- bias_out: float32 [16, 256], P('gx'), may hold values from -3 to 3
Outputs:
- fields_next: float32 [128, 256, 256], P(('group', 'gx')), parts along dimension 0
The draws below stay inside these ranges and needn't reach their ends.
There are 2 independent parts, one for each index of `group`. The reference program is written for one: setup_inputs(seed, part) draws one part's arguments, and reference() takes and returns one part's arrays. A program takes and returns all parts, laid end to end along the dimension named above; an argument that names none is the same for every part. Nothing has to cross between parts.
Inputs may be any that keep to these rules, and one draw needn't show every extreme that they name: `strip_table`: never falls along the rows; every band holds 1 to 32 consecutive rows, and some band exactly 32.
All inputs are finite; a program needn't handle non-finite values. No bound on the sum of `switches` on one device may be relied on, other than what follows from the above.
Results may differ from the reference program's by a relative error of at most 0.0028.
Values may be sent and summed in bfloat16 or wider, within the bound.
No kernel may reach another device: no remote copies, remote signals or barrier semaphores. Data moves between devices by JAX's collectives and lax.ppermute only.
A program may use at most 64 MiB of HBM per device.

```python
import math
import jax
import jax.numpy as jnp
import numpy as np
from jax import lax

F = 4
LEV = 64
H = 256
LAT = 256
LON_DEV = 4
TL = 1
STEPS = 1
C = 256
LON = 64
TILES_DEV = 256
STRIPS = 16
CAP = 32
SECTIONS = 2
N_GX = 16


def plant(array, key, low, high):
    spot = [jax.random.randint(jax.random.fold_in(key, axis), (), 0, length) for axis, length in enumerate(array.shape)]
    main_axis = array.shape.index(max(array.shape))
    beside = spot[:main_axis] + [(spot[main_axis] + 1) % array.shape[main_axis]] + spot[main_axis + 1:]
    return array.at[tuple(spot)].set(low).at[tuple(beside)].set(high)


def block_levels(own_key, dims, cuts, low, top_value):
    loudness = 1.0
    for dim, blocks in cuts:
        steps = jax.random.uniform(jax.random.fold_in(jax.random.fold_in(own_key, 6), dim), (blocks,), jnp.float32, low / len(cuts), top_value / len(cuts))
        loudness = loudness * jnp.repeat(jnp.exp(steps), dims[dim] // blocks).reshape((-1,) + (1,) * (len(dims) - 1 - dim))
    return loudness


def profile(count, total, most, lean):
    portions = [(1 << 20) // math.isqrt(standing ** lean) + 1 for standing in range(2, count + 1)]
    surplus, given = total - most - (count - 1), [1] * (count - 1)
    while surplus > 0:
        candidates = [i for i in range(count - 1) if given[i] < most]
        mass, left = sum([portions[i] for i in candidates]), surplus
        for i in candidates:
            more = min(most - given[i], max(1, left * portions[i] // mass), surplus)
            given[i] = given[i] + more
            surplus = surplus - more
    return np.array([most] + given)


def ragged(rng, number_of, total, most, skew):
    if number_of == 2:
        one = jax.random.randint(rng, (), max(1, total - most), min(most, total - 1) + 1)
        return jnp.stack([one, total - one])
    tallies = jnp.asarray(profile(number_of, total, most, skew), jnp.int32)
    couples = (number_of - 1) // 2
    source_of, sink = tallies[1:1 + 2 * couples:2], tallies[2:2 + 2 * couples:2]
    margin = jnp.minimum(source_of - 1, most - sink)
    moved = jax.random.randint(jax.random.fold_in(rng, 1), (couples,), 0, 1 << 20) % (margin + 1)
    tallies = tallies.at[1:1 + 2 * couples:2].set(source_of - moved).at[2:2 + 2 * couples:2].set(sink + moved)
    return tallies[jax.random.permutation(jax.random.fold_in(rng, 2), number_of)]


def bell_draw(rng, dims, scale, bound, pieces=(), held_as=jnp.bfloat16):
    entries = scale * jax.random.normal(rng, dims, jnp.float32)
    if pieces:
        entries = entries * block_levels(rng, dims, pieces, -0.22, 0.18)
    return jnp.clip(entries, -bound, bound).astype(held_as)


def setup_inputs(seed: int = 0, part: int = 0) -> dict:
    key_of = jax.random.split(jax.random.key(seed), 11)
    part_keys = jax.random.split(jax.random.fold_in(key_of[10], part), 11)
    fields = bell_draw(part_keys[0], (LON, LAT, C), 1.0, 6.0, ((0, 16),), jnp.float32)
    courant = jnp.clip(jax.random.uniform(part_keys[1], (LON, LAT * LEV), jnp.float32, -0.8, 0.8) * block_levels(part_keys[1], (LON, LAT * LEV), ((0, 16),), -0.4, 0.0), -0.8, 0.8)
    switches = plant((jax.random.randint(part_keys[2], (SECTIONS, LON, LAT * LEV), 0, 2) < 1).astype(jnp.int32), jax.random.fold_in(part_keys[2], 1), 0, 1)
    strip_table = jnp.searchsorted(jnp.cumsum(ragged(part_keys[3], STRIPS, TILES_DEV, CAP, 2)), jnp.arange(TILES_DEV), side="right").astype(jnp.int32)
    weight_in = bell_draw(key_of[4], (9 * C, H), (9 * C) ** -0.5, 0.125)
    bias_in = bell_draw(key_of[5], (H,), 0.5, 3.0, (), jnp.float32)
    weight_mid = bell_draw(key_of[6], (STRIPS, H, H), H ** -0.5, 0.375, ((0, 16),))
    bias_mid = bell_draw(key_of[7], (STRIPS, H), 0.5, 3.0, ((0, 16),), jnp.float32)
    weight_out = bell_draw(key_of[8], (STRIPS, H, C), H ** -0.5, 0.375, ((0, 16),))
    bias_out = bell_draw(key_of[9], (STRIPS, C), 0.5, 3.0, ((0, 16),), jnp.float32)
    return {"fields": fields, "courant": courant, "switches": switches, "strip_table": strip_table, "weight_in": weight_in, "bias_in": bias_in, "weight_mid": weight_mid, "bias_mid": bias_mid, "weight_out": weight_out, "bias_out": bias_out}


def flux_change(values, speeds, switch_now):
    right_vals = jnp.roll(values, -1, 0)
    damping = switch_now * speeds * speeds + (1.0 - switch_now) * jnp.abs(speeds)
    face_flux = 0.5 * speeds * (values + right_vals) - 0.5 * damping * (right_vals - values)
    return face_flux - jnp.roll(face_flux, 1, 0)


def column_tendency(current, strip_table, weight_in, bias_in, weight_mid, bias_mid, weight_out, bias_out):
    columns_bf = current.astype(jnp.bfloat16)
    columns_bf = jnp.concatenate([columns_bf[-1:], columns_bf, columns_bf[:1]], 0)
    columns_bf = jnp.pad(columns_bf, ((0, 0), (1, 1), (0, 0)))
    weights = weight_in.reshape(3, 3, C, H)
    summed = jnp.zeros((LON * LAT, H), jnp.float32)
    for lon_off in range(3):
        for lat_off in range(3):
            window = columns_bf[lon_off:lon_off + LON, lat_off:lat_off + LAT].reshape(-1, C)
            summed = summed + jnp.dot(window, weights[lon_off, lat_off], preferred_element_type=jnp.float32)
    hidden_one = jax.nn.silu(summed + bias_in).astype(jnp.bfloat16)
    hidden_one = hidden_one.reshape(N_GX, LON_DEV, TILES_DEV, TL, H).transpose(0, 2, 1, 3, 4)
    hidden_one = hidden_one.reshape(N_GX, TILES_DEV, LON_DEV * TL, H)
    strips = jnp.broadcast_to(strip_table[None, :], (N_GX, TILES_DEV))

    def apply_strips(payload):
        tile_block, chosen = payload
        middle = jnp.einsum("tph,thk->tpk", tile_block.astype(jnp.float32), weight_mid[chosen].astype(jnp.float32))
        hidden_two = jax.nn.silu(middle + bias_mid[chosen][:, None, :]).astype(jnp.bfloat16)
        result = jnp.einsum("tph,thk->tpk", hidden_two.astype(jnp.float32), weight_out[chosen].astype(jnp.float32))
        return (result + bias_out[chosen][:, None, :]).astype(jnp.bfloat16)

    tendency = lax.map(apply_strips, (hidden_one, strips))
    tendency = tendency.reshape(N_GX, TILES_DEV, LON_DEV, TL, C).transpose(0, 2, 1, 3, 4)
    return tendency.reshape(LON, LAT, C)


def reference(fields, courant, switches, strip_table, weight_in, bias_in, weight_mid, bias_mid, weight_out, bias_out):
    speeds = courant.reshape(LON, LAT, 1, LEV)
    current = fields
    for step_index in range(STEPS):
        tendency = column_tendency(current, strip_table, weight_in, bias_in, weight_mid, bias_mid, weight_out, bias_out)
        layered = current.reshape(LON, LAT, F, LEV)
        switch_one = switches[2 * step_index].reshape(LON, LAT, 1, LEV).astype(jnp.float32)
        switch_two = switches[2 * step_index + 1].reshape(LON, LAT, 1, LEV).astype(jnp.float32)
        section_one = layered - flux_change(layered, speeds, switch_one)
        moved = 0.5 * layered + 0.5 * (section_one - flux_change(section_one, speeds, switch_two))
        current = moved.reshape(LON, LAT, C) + tendency.astype(jnp.float32)
    return current
```

```python
import functools

import jax
import jax.numpy as jnp
from jax import lax
from jax.experimental import pallas as pl
from jax.experimental.pallas import tpu as pltpu
from jax.sharding import PartitionSpec as P


def passed_along(array, axis, by):
    length = lax.axis_size(axis)
    return lax.ppermute(array, axis, [(i, (i + by) % length) for i in range(length)])


def face_flux(left_vals, right_vals, speeds, switch_now):
    damping = switch_now * speeds * speeds + (1.0 - switch_now) * jnp.abs(speeds)
    return 0.5 * speeds * (left_vals + right_vals) - 0.5 * damping * (right_vals - left_vals)


def flux_change(values, right_col, speeds, switch_now):
    right_vals = jnp.concatenate([values[1:], right_col], 0)
    edge_flux = face_flux(values, right_vals, speeds, switch_now)
    left_flux = passed_along(edge_flux[-1:].astype(jnp.bfloat16), "gx", 1).astype(jnp.float32)
    return edge_flux - jnp.concatenate([left_flux, edge_flux[:-1]], 0)


def band_kernel(tile_ref, band_ref, valid_ref, h1_ref, bid_ref, wm_ref, bm_ref, wo_ref, bo_ref, out_ref):
    step = pl.program_id(0)
    band = band_ref[step]
    first = jnp.logical_or(step == 0, tile_ref[step] != tile_ref[jnp.maximum(step - 1, 0)])

    @pl.when(first)
    def _():
        out_ref[...] = jnp.zeros_like(out_ref)

    @pl.when(valid_ref[step] == 1)
    def _():
        lon, rows, hidden = h1_ref.shape
        block = h1_ref[...].reshape(lon * rows, hidden)
        middle = jnp.dot(block, wm_ref[0], preferred_element_type=jnp.float32) + bm_ref[0]
        hidden_two = (middle / (1.0 + jnp.exp(-middle))).astype(jnp.bfloat16)
        result = jnp.dot(hidden_two, wo_ref[0], preferred_element_type=jnp.float32) + bo_ref[0]
        result = result.astype(jnp.bfloat16).astype(jnp.float32)
        result = result.reshape(lon, rows, result.shape[-1])
        mask = (bid_ref[...] == band)[None]
        out_ref[...] = jnp.where(mask, result, out_ref[...])


def band_networks(hidden_one, strip_table, weight_mid, bias_mid, weight_out, bias_out, tile_rows):
    lon, lat_rows, hidden = hidden_one.shape
    channels = weight_out.shape[-1]
    bands = weight_mid.shape[0]
    tiles = lat_rows // tile_rows
    steps = tiles + bands - 1
    low = strip_table[0::tile_rows]
    high = strip_table[tile_rows - 1 :: tile_rows]
    count = high - low + 1
    offset = jnp.cumsum(count) - count
    total = jnp.sum(count)
    index = jnp.arange(steps, dtype=jnp.int32)
    tile = jnp.clip(jnp.searchsorted(offset, index, side="right").astype(jnp.int32) - 1, 0, tiles - 1)
    band = low[tile] + (index - offset[tile])
    valid = index < total
    tile = jnp.where(valid, tile, tiles - 1).astype(jnp.int32)
    band = jnp.clip(jnp.where(valid, band, high[tiles - 1]), 0, bands - 1).astype(jnp.int32)
    valid = valid.astype(jnp.int32)
    band_ids = strip_table.reshape(lat_rows, 1)
    grid_spec = pltpu.PrefetchScalarGridSpec(
        num_scalar_prefetch=3,
        grid=(steps,),
        in_specs=[
            pl.BlockSpec((lon, tile_rows, hidden), lambda s, t, b, v: (0, t[s], 0)),
            pl.BlockSpec((tile_rows, 1), lambda s, t, b, v: (t[s], 0)),
            pl.BlockSpec((1, hidden, hidden), lambda s, t, b, v: (b[s], 0, 0)),
            pl.BlockSpec((1, 1, hidden), lambda s, t, b, v: (b[s], 0, 0)),
            pl.BlockSpec((1, hidden, channels), lambda s, t, b, v: (b[s], 0, 0)),
            pl.BlockSpec((1, 1, channels), lambda s, t, b, v: (b[s], 0, 0)),
        ],
        out_specs=pl.BlockSpec((lon, tile_rows, channels), lambda s, t, b, v: (0, t[s], 0)),
    )
    return pl.pallas_call(
        band_kernel,
        grid_spec=grid_spec,
        out_shape=jax.ShapeDtypeStruct((lon, lat_rows, channels), jnp.float32),
        compiler_params=pltpu.CompilerParams(dimension_semantics=("arbitrary",)),
    )(
        tile,
        band,
        valid,
        hidden_one,
        band_ids,
        weight_mid,
        bias_mid.reshape(bands, 1, hidden),
        weight_out,
        bias_out.reshape(bands, 1, channels),
    )


def on_device(
    fields,
    courant,
    switches,
    strip_table,
    weight_in,
    bias_in,
    weight_mid,
    bias_mid,
    weight_out,
    bias_out,
):
    lon_dev, lat_rows, channels = fields.shape
    levels = courant.shape[1] // lat_rows
    field_count = channels // levels
    hidden = weight_in.shape[1]
    tile_rows = min(32, lat_rows)

    all_mid = lax.all_gather(weight_mid, "gx", axis=0, tiled=True)
    all_bmid = lax.all_gather(bias_mid, "gx", axis=0, tiled=True)
    all_out = lax.all_gather(weight_out, "gx", axis=0, tiled=True)
    all_bout = lax.all_gather(bias_out, "gx", axis=0, tiled=True)

    columns_bf = fields.astype(jnp.bfloat16)
    west_col = passed_along(columns_bf[-1:], "gx", 1)
    east_col = passed_along(columns_bf[:1], "gx", -1)
    padded = jnp.concatenate([west_col, columns_bf, east_col], 0)
    padded = jnp.pad(padded, ((0, 0), (1, 1), (0, 0)))
    kernel = weight_in.reshape(3, 3, channels, hidden)
    summed = lax.conv_general_dilated(
        padded[None],
        kernel,
        (1, 1),
        "VALID",
        dimension_numbers=("NHWC", "HWIO", "NHWC"),
        preferred_element_type=jnp.float32,
    )[0]
    summed = summed + bias_in
    hidden_one = jax.nn.silu(summed).astype(jnp.bfloat16)

    tendency = band_networks(hidden_one, strip_table, all_mid, all_bmid, all_out, all_bout, tile_rows)

    speeds = courant.reshape(lon_dev, lat_rows, 1, levels)
    layered = fields.reshape(lon_dev, lat_rows, field_count, levels)
    switch_one = switches[0].reshape(lon_dev, lat_rows, 1, levels).astype(jnp.float32)
    switch_two = switches[1].reshape(lon_dev, lat_rows, 1, levels).astype(jnp.float32)
    ahead_col = east_col.astype(jnp.float32).reshape(1, lat_rows, field_count, levels)
    section_one = layered - flux_change(layered, ahead_col, speeds, switch_one)
    ahead_two = passed_along(section_one[:1].astype(jnp.bfloat16), "gx", -1).astype(jnp.float32)
    section_two = section_one - flux_change(section_one, ahead_two, speeds, switch_two)
    moved = 0.5 * layered + 0.5 * section_two
    return moved.reshape(lon_dev, lat_rows, channels) + tendency


def solution(mesh):
    return jax.shard_map(
        on_device,
        mesh=mesh,
        in_specs=(
            P(("group", "gx"), None, None),
            P(("group", "gx"), None),
            P(None, ("group", "gx"), None),
            P("group"),
            P(),
            P(),
            P("gx", None, None),
            P("gx", None),
            P("gx", None, None),
            P("gx", None),
        ),
        out_specs=P(("group", "gx"), None, None),
        check_vma=False,
    )
```

```python
import jax
import jax.numpy as jnp
from jax import lax
from jax.experimental import pallas as pl
from jax.experimental.pallas import tpu as pltpu
from jax.sharding import PartitionSpec as P

BIAS_ROWS = 16


def passed_along(array, axis, by):
    length = lax.axis_size(axis)
    return lax.ppermute(array, axis, [(i, (i + by) % length) for i in range(length)])


def split_three(values):
    high = values.astype(jnp.bfloat16)
    rest = values - high.astype(jnp.float32)
    middle = rest.astype(jnp.bfloat16)
    low = (rest - middle.astype(jnp.float32)).astype(jnp.bfloat16)
    return [high, middle, low]


def pack_band(weight_mid, bias_mid, weight_out, bias_out):
    hidden = weight_mid.shape[-1]
    rows = split_three(bias_mid[0]) + split_three(bias_out[0])
    rows = jnp.stack(rows, 0)
    rows = jnp.pad(rows, ((0, BIAS_ROWS - rows.shape[0]), (0, 0)))
    return jnp.concatenate([weight_mid[0], weight_out[0], rows], 0)[None]


def face_flux(left_vals, right_vals, speeds, switch_now):
    damping = switch_now * speeds * speeds + (1.0 - switch_now) * jnp.abs(speeds)
    return 0.5 * speeds * (left_vals + right_vals) - 0.5 * damping * (right_vals - left_vals)


def flux_change(values, right_col, speeds, switch_now):
    right_vals = jnp.concatenate([values[1:], right_col], 0)
    edge_flux = face_flux(values, right_vals, speeds, switch_now)
    left_flux = passed_along(edge_flux[-1:].astype(jnp.bfloat16), "gx", 1).astype(jnp.float32)
    return edge_flux - jnp.concatenate([left_flux, edge_flux[:-1]], 0)


def band_kernel(tile_ref, slot_ref, band_ref, valid_ref, h1_ref, bid_ref, wm_ref, wo_ref, b_ref, out_ref):
    step = pl.program_id(0)
    band = band_ref[step]
    first = jnp.logical_or(step == 0, tile_ref[step] != tile_ref[jnp.maximum(step - 1, 0)])

    @pl.when(first)
    def _():
        out_ref[...] = jnp.zeros_like(out_ref)

    @pl.when(valid_ref[step] == 1)
    def _():
        lon, rows, hidden = h1_ref.shape
        parts = b_ref[0].astype(jnp.float32)
        bias_mid = (parts[0:1] + parts[1:2]) + parts[2:3]
        bias_out = (parts[3:4] + parts[4:5]) + parts[5:6]
        block = h1_ref[...].reshape(lon * rows, hidden)
        middle = jnp.dot(block, wm_ref[0], preferred_element_type=jnp.float32) + bias_mid
        hidden_two = (middle / (1.0 + jnp.exp(-middle))).astype(jnp.bfloat16)
        result = jnp.dot(hidden_two, wo_ref[0], preferred_element_type=jnp.float32) + bias_out
        result = result.astype(jnp.bfloat16).astype(jnp.float32)
        result = result.reshape(lon, rows, result.shape[-1])
        mask = (bid_ref[...] == band)[None]
        out_ref[...] = jnp.where(mask, result, out_ref[...])


def band_networks(hidden_one, strip_table, packed, tile_rows):
    lon, lat_rows, hidden = hidden_one.shape
    channels = packed.shape[-1]
    bands = packed.shape[0]
    me = lax.axis_index("gx")
    tiles = lat_rows // tile_rows
    steps = tiles + bands - 1
    low = strip_table[0::tile_rows]
    high = strip_table[tile_rows - 1 :: tile_rows]
    count = high - low + 1
    offset = jnp.cumsum(count) - count
    total = jnp.sum(count)
    index = jnp.arange(steps, dtype=jnp.int32)
    started = (offset[None, :] <= index[:, None]).astype(jnp.int32)
    tile = jnp.clip(jnp.sum(started, 1) - 1, 0, tiles - 1)
    pick = (tile[:, None] == jnp.arange(tiles, dtype=jnp.int32)[None, :]).astype(jnp.int32)
    band = jnp.sum(pick * low[None, :], 1) + index - jnp.sum(pick * offset[None, :], 1)
    valid = index < total
    tile = jnp.where(valid, tile, tiles - 1).astype(jnp.int32)
    band = jnp.clip(jnp.where(valid, band, high[tiles - 1]), 0, bands - 1).astype(jnp.int32)
    slot = band
    valid = valid.astype(jnp.int32)
    band_ids = strip_table.reshape(lat_rows, 1)
    del me
    grid_spec = pltpu.PrefetchScalarGridSpec(
        num_scalar_prefetch=4,
        grid=(steps,),
        in_specs=[
            pl.BlockSpec((lon, tile_rows, hidden), lambda s, t, k, b, v: (0, t[s], 0)),
            pl.BlockSpec((tile_rows, 1), lambda s, t, k, b, v: (t[s], 0)),
            pl.BlockSpec((1, hidden, hidden), lambda s, t, k, b, v: (k[s], 0, 0)),
            pl.BlockSpec((1, hidden, channels), lambda s, t, k, b, v: (k[s], 1, 0)),
            pl.BlockSpec((1, BIAS_ROWS, channels), lambda s, t, k, b, v: (k[s], 2 * hidden // BIAS_ROWS, 0)),
        ],
        out_specs=pl.BlockSpec((lon, tile_rows, channels), lambda s, t, k, b, v: (0, t[s], 0)),
    )
    return pl.pallas_call(
        band_kernel,
        grid_spec=grid_spec,
        out_shape=jax.ShapeDtypeStruct((lon, lat_rows, channels), jnp.float32),
        compiler_params=pltpu.CompilerParams(dimension_semantics=("arbitrary",)),
    )(tile, slot, band, valid, hidden_one, band_ids, packed, packed, packed)


def widened(values, field_count):
    lon, rows, levels = values.shape
    return jnp.broadcast_to(values[:, :, None, :], (lon, rows, field_count, levels)).reshape(
        lon, rows, field_count * levels
    )


def on_device(
    fields,
    courant,
    switches,
    strip_table,
    weight_in,
    bias_in,
    weight_mid,
    bias_mid,
    weight_out,
    bias_out,
):
    lon_dev, lat_rows, channels = fields.shape
    levels = courant.shape[1] // lat_rows
    field_count = channels // levels
    hidden = weight_in.shape[1]
    tile_rows = min(32, lat_rows)

    packed = pack_band(weight_mid, bias_mid, weight_out, bias_out)
    packed = lax.all_gather(packed, "gx", axis=0, tiled=True)

    columns_bf = fields.astype(jnp.bfloat16)
    west_col = passed_along(columns_bf[-1:], "gx", 1)
    east_col = passed_along(columns_bf[:1], "gx", -1)
    padded = jnp.concatenate([west_col, columns_bf, east_col], 0)
    padded = jnp.pad(padded, ((0, 0), (1, 1), (0, 0)))
    kernel = weight_in.reshape(3, 3, channels, hidden)
    summed = lax.conv_general_dilated(
        padded[None],
        kernel,
        (1, 1),
        "VALID",
        dimension_numbers=("NHWC", "HWIO", "NHWC"),
        preferred_element_type=jnp.float32,
    )[0]
    summed = summed + bias_in
    hidden_one = jax.nn.silu(summed).astype(jnp.bfloat16)

    tendency = band_networks(hidden_one, strip_table, packed, tile_rows)

    speeds = widened(courant.reshape(lon_dev, lat_rows, levels), field_count)
    switch_one = widened(switches[0].reshape(lon_dev, lat_rows, levels).astype(jnp.float32), field_count)
    switch_two = widened(switches[1].reshape(lon_dev, lat_rows, levels).astype(jnp.float32), field_count)
    ahead_col = east_col.astype(jnp.float32)
    section_one = fields - flux_change(fields, ahead_col, speeds, switch_one)
    ahead_two = passed_along(section_one[:1].astype(jnp.bfloat16), "gx", -1).astype(jnp.float32)
    section_two = section_one - flux_change(section_one, ahead_two, speeds, switch_two)
    moved = 0.5 * fields + 0.5 * section_two
    return moved + tendency


def solution(mesh):
    return jax.shard_map(
        on_device,
        mesh=mesh,
        in_specs=(
            P(("group", "gx"), None, None),
            P(("group", "gx"), None),
            P(None, ("group", "gx"), None),
            P("group"),
            P(),
            P(),
            P("gx", None, None),
            P("gx", None),
            P("gx", None, None),
            P("gx", None),
        ),
        out_specs=P(("group", "gx"), None, None),
        check_vma=False,
    )
```

```python
import jax
import jax.numpy as jnp
from jax import lax
from jax.experimental import pallas as pl
from jax.experimental.pallas import tpu as pltpu
from jax.sharding import PartitionSpec as P

BIAS_ROWS = 16


def passed_along(array, axis, by):
    length = lax.axis_size(axis)
    return lax.ppermute(array, axis, [(i, (i + by) % length) for i in range(length)])


def split_three(values):
    high = values.astype(jnp.bfloat16)
    rest = values - high.astype(jnp.float32)
    middle = rest.astype(jnp.bfloat16)
    low = (rest - middle.astype(jnp.float32)).astype(jnp.bfloat16)
    return [high, middle, low]


def pack_band(weight_mid, bias_mid, weight_out, bias_out):
    hidden = weight_mid.shape[-1]
    rows = split_three(bias_mid[0]) + split_three(bias_out[0])
    rows = jnp.stack(rows, 0)
    rows = jnp.pad(rows, ((0, BIAS_ROWS - rows.shape[0]), (0, 0)))
    return jnp.concatenate([weight_mid[0], weight_out[0], rows], 0)[None]


def gather_bands(packed):
    devices = lax.axis_size("gx")
    half = devices // 2
    same = [packed]
    for k in range(1, half):
        same.append(lax.ppermute(packed, "gx", [(i, (i + 2 * k) % devices) for i in range(devices)]))
    swap = [(i, i ^ 1) for i in range(devices)]
    other = [lax.ppermute(piece, "gx", swap) for piece in same]
    return jnp.concatenate(same + other, 0)


def slot_of(band):
    devices = lax.axis_size("gx")
    half = devices // 2
    me = lax.axis_index("gx")
    mine = (band % 2) == (me % 2)
    base = jnp.where(mine, me, me ^ 1)
    return jnp.where(mine, 0, half) + ((base - band) % devices) // 2


def face_flux(left_vals, right_vals, speeds, switch_now):
    damping = switch_now * speeds * speeds + (1.0 - switch_now) * jnp.abs(speeds)
    return 0.5 * speeds * (left_vals + right_vals) - 0.5 * damping * (right_vals - left_vals)


def flux_change(values, right_col, speeds, switch_now):
    right_vals = jnp.concatenate([values[1:], right_col], 0)
    edge_flux = face_flux(values, right_vals, speeds, switch_now)
    left_flux = passed_along(edge_flux[-1:].astype(jnp.bfloat16), "gx", 1).astype(jnp.float32)
    return edge_flux - jnp.concatenate([left_flux, edge_flux[:-1]], 0)


def band_kernel(tile_ref, slot_ref, band_ref, valid_ref, h1_ref, bid_ref, wm_ref, wo_ref, b_ref, out_ref):
    step = pl.program_id(0)
    band = band_ref[step]
    first = jnp.logical_or(step == 0, tile_ref[step] != tile_ref[jnp.maximum(step - 1, 0)])

    @pl.when(first)
    def _():
        out_ref[...] = jnp.zeros_like(out_ref)

    @pl.when(valid_ref[step] == 1)
    def _():
        lon, rows, hidden = h1_ref.shape
        parts = b_ref[0].astype(jnp.float32)
        bias_mid = (parts[0:1] + parts[1:2]) + parts[2:3]
        bias_out = (parts[3:4] + parts[4:5]) + parts[5:6]
        block = h1_ref[...].reshape(lon * rows, hidden)
        middle = jnp.dot(block, wm_ref[0], preferred_element_type=jnp.float32) + bias_mid
        hidden_two = (middle / (1.0 + jnp.exp(-middle))).astype(jnp.bfloat16)
        result = jnp.dot(hidden_two, wo_ref[0], preferred_element_type=jnp.float32) + bias_out
        result = result.astype(jnp.bfloat16).astype(jnp.float32)
        result = result.reshape(lon, rows, result.shape[-1])
        mask = (bid_ref[...] == band)[None]
        out_ref[...] = jnp.where(mask, result, out_ref[...])


def band_networks(hidden_one, strip_table, packed, tile_rows):
    lon, lat_rows, hidden = hidden_one.shape
    channels = packed.shape[-1]
    bands = packed.shape[0]
    tiles = lat_rows // tile_rows
    steps = tiles + bands - 1
    low = strip_table[0::tile_rows]
    high = strip_table[tile_rows - 1 :: tile_rows]
    count = high - low + 1
    offset = jnp.cumsum(count) - count
    total = jnp.sum(count)
    index = jnp.arange(steps, dtype=jnp.int32)
    started = (offset[None, :] <= index[:, None]).astype(jnp.int32)
    tile = jnp.clip(jnp.sum(started, 1) - 1, 0, tiles - 1)
    pick = (tile[:, None] == jnp.arange(tiles, dtype=jnp.int32)[None, :]).astype(jnp.int32)
    band = jnp.sum(pick * low[None, :], 1) + index - jnp.sum(pick * offset[None, :], 1)
    valid = index < total
    tile = jnp.where(valid, tile, tiles - 1).astype(jnp.int32)
    band = jnp.clip(jnp.where(valid, band, high[tiles - 1]), 0, bands - 1).astype(jnp.int32)
    slot = slot_of(band).astype(jnp.int32)
    valid = valid.astype(jnp.int32)
    band_ids = strip_table.reshape(lat_rows, 1)
    grid_spec = pltpu.PrefetchScalarGridSpec(
        num_scalar_prefetch=4,
        grid=(steps,),
        in_specs=[
            pl.BlockSpec((lon, tile_rows, hidden), lambda s, t, k, b, v: (0, t[s], 0)),
            pl.BlockSpec((tile_rows, 1), lambda s, t, k, b, v: (t[s], 0)),
            pl.BlockSpec((1, hidden, hidden), lambda s, t, k, b, v: (k[s], 0, 0)),
            pl.BlockSpec((1, hidden, channels), lambda s, t, k, b, v: (k[s], 1, 0)),
            pl.BlockSpec((1, BIAS_ROWS, channels), lambda s, t, k, b, v: (k[s], 2 * hidden // BIAS_ROWS, 0)),
        ],
        out_specs=pl.BlockSpec((lon, tile_rows, channels), lambda s, t, k, b, v: (0, t[s], 0)),
    )
    return pl.pallas_call(
        band_kernel,
        grid_spec=grid_spec,
        out_shape=jax.ShapeDtypeStruct((lon, lat_rows, channels), jnp.float32),
        compiler_params=pltpu.CompilerParams(dimension_semantics=("arbitrary",)),
    )(tile, slot, band, valid, hidden_one, band_ids, packed, packed, packed)


def widened(values, field_count):
    lon, rows, levels = values.shape
    return jnp.broadcast_to(values[:, :, None, :], (lon, rows, field_count, levels)).reshape(
        lon, rows, field_count * levels
    )


def on_device(
    fields,
    courant,
    switches,
    strip_table,
    weight_in,
    bias_in,
    weight_mid,
    bias_mid,
    weight_out,
    bias_out,
):
    lon_dev, lat_rows, channels = fields.shape
    levels = courant.shape[1] // lat_rows
    field_count = channels // levels
    hidden = weight_in.shape[1]
    tile_rows = min(32, lat_rows)

    packed = pack_band(weight_mid, bias_mid, weight_out, bias_out)
    packed = gather_bands(packed)

    columns_bf = fields.astype(jnp.bfloat16)
    west_col = passed_along(columns_bf[-1:], "gx", 1)
    east_col = passed_along(columns_bf[:1], "gx", -1)
    padded = jnp.concatenate([west_col, columns_bf, east_col], 0)
    padded = jnp.pad(padded, ((0, 0), (1, 1), (0, 0)))
    kernel = weight_in.reshape(3, 3, channels, hidden)
    summed = lax.conv_general_dilated(
        padded[None],
        kernel,
        (1, 1),
        "VALID",
        dimension_numbers=("NHWC", "HWIO", "NHWC"),
        preferred_element_type=jnp.float32,
    )[0]
    summed = summed + bias_in
    hidden_one = jax.nn.silu(summed).astype(jnp.bfloat16)

    tendency = band_networks(hidden_one, strip_table, packed, tile_rows)

    speeds = widened(courant.reshape(lon_dev, lat_rows, levels), field_count)
    switch_one = widened(switches[0].reshape(lon_dev, lat_rows, levels).astype(jnp.float32), field_count)
    switch_two = widened(switches[1].reshape(lon_dev, lat_rows, levels).astype(jnp.float32), field_count)
    ahead_col = east_col.astype(jnp.float32)
    section_one = fields - flux_change(fields, ahead_col, speeds, switch_one)
    ahead_two = passed_along(section_one[:1].astype(jnp.bfloat16), "gx", -1).astype(jnp.float32)
    section_two = section_one - flux_change(section_one, ahead_two, speeds, switch_two)
    moved = 0.5 * fields + 0.5 * section_two
    return moved + tendency


def solution(mesh):
    return jax.shard_map(
        on_device,
        mesh=mesh,
        in_specs=(
            P(("group", "gx"), None, None),
            P(("group", "gx"), None),
            P(None, ("group", "gx"), None),
            P("group"),
            P(),
            P(),
            P("gx", None, None),
            P("gx", None),
            P("gx", None, None),
            P("gx", None),
        ),
        out_specs=P(("group", "gx"), None, None),
        check_vma=False,
    )
```

```python
import jax
import jax.numpy as jnp
from jax import lax
from jax.experimental import pallas as pl
from jax.experimental.pallas import tpu as pltpu
from jax.sharding import PartitionSpec as P

BIAS_ROWS = 16
ALIGN = 16


def passed_along(array, axis, by):
    length = lax.axis_size(axis)
    return lax.ppermute(array, axis, [(i, (i + by) % length) for i in range(length)])


def split_three(values):
    high = values.astype(jnp.bfloat16)
    rest = values - high.astype(jnp.float32)
    middle = rest.astype(jnp.bfloat16)
    low = (rest - middle.astype(jnp.float32)).astype(jnp.bfloat16)
    return [high, middle, low]


def pack_layer(weight, bias):
    rows = jnp.stack(split_three(bias[0]), 0)
    rows = jnp.pad(rows, ((0, BIAS_ROWS - rows.shape[0]), (0, 0)))
    return jnp.concatenate([weight[0], rows], 0)[None]


def face_flux(left_vals, right_vals, speeds, switch_now):
    damping = switch_now * speeds * speeds + (1.0 - switch_now) * jnp.abs(speeds)
    return 0.5 * speeds * (left_vals + right_vals) - 0.5 * damping * (right_vals - left_vals)


def flux_change(values, right_col, speeds, switch_now):
    right_vals = jnp.concatenate([values[1:], right_col], 0)
    edge_flux = face_flux(values, right_vals, speeds, switch_now)
    left_flux = passed_along(edge_flux[-1:].astype(jnp.bfloat16), "gx", 1).astype(jnp.float32)
    return edge_flux - jnp.concatenate([left_flux, edge_flux[:-1]], 0)


def make_band_kernel(window, activate):
    def kernel(lo_ref, hi_ref, win_ref, x_ref, w_hbm, out_ref, acc_ref, wbuf, sem):
        bands = w_hbm.shape[0]
        inner = w_hbm.shape[1] - BIAS_ROWS

        def fetch(band, slot):
            return pltpu.make_async_copy(w_hbm.at[band], wbuf.at[slot], sem.at[slot])

        fetch(0, 0).start()
        acc_ref[...] = jnp.zeros_like(acc_ref)

        def body(band, carry):
            slot = band % 2

            @pl.when(band + 1 < bands)
            def _():
                fetch(band + 1, 1 - slot).start()

            fetch(band, slot).wait()
            start = pl.multiple_of(win_ref[band], ALIGN)
            block = x_ref[pl.ds(start, window), :]
            weight = wbuf[slot, 0:inner, :]
            parts = wbuf[slot, inner : inner + 3, :].astype(jnp.float32)
            bias = (parts[0:1] + parts[1:2]) + parts[2:3]
            value = jnp.dot(block, weight, preferred_element_type=jnp.float32) + bias
            if not activate:
                value = value.astype(jnp.bfloat16).astype(jnp.float32)
            rows = start + lax.broadcasted_iota(jnp.int32, (window, 1), 0)
            mask = jnp.logical_and(rows >= lo_ref[band], rows < hi_ref[band])
            acc_ref[pl.ds(start, window), :] = jnp.where(mask, value, acc_ref[pl.ds(start, window), :])
            return carry

        lax.fori_loop(0, bands, body, 0)
        total = acc_ref[...]
        if activate:
            out_ref[...] = (total / (1.0 + jnp.exp(-total))).astype(out_ref.dtype)
        else:
            out_ref[...] = total.astype(out_ref.dtype)

    return kernel


def band_layer(x, packed, lo, hi, win, window, activate, out_dtype):
    rows, _ = x.shape
    channels = packed.shape[-1]
    smem = pl.BlockSpec(memory_space=pltpu.SMEM)
    return pl.pallas_call(
        make_band_kernel(window, activate),
        in_specs=[smem, smem, smem, pl.BlockSpec(memory_space=pltpu.VMEM), pl.BlockSpec(memory_space=pl.ANY)],
        out_specs=pl.BlockSpec(memory_space=pltpu.VMEM),
        out_shape=jax.ShapeDtypeStruct((rows, channels), out_dtype),
        scratch_shapes=[
            pltpu.VMEM((rows, channels), jnp.float32),
            pltpu.VMEM((2,) + packed.shape[1:], packed.dtype),
            pltpu.SemaphoreType.DMA((2,)),
        ],
    )(lo, hi, win, x, packed)


def widened(values, field_count):
    lon, rows, levels = values.shape
    return jnp.broadcast_to(values[:, :, None, :], (lon, rows, field_count, levels)).reshape(
        lon, rows, field_count * levels
    )


def on_device(
    fields,
    courant,
    switches,
    strip_table,
    weight_in,
    bias_in,
    weight_mid,
    bias_mid,
    weight_out,
    bias_out,
):
    lon_dev, lat_rows, channels = fields.shape
    levels = courant.shape[1] // lat_rows
    field_count = channels // levels
    hidden = weight_in.shape[1]
    devices = lax.axis_size("gx")
    capacity = max(2, 2 * lat_rows // devices)
    rows = lat_rows * lon_dev
    window = min(rows, lon_dev * capacity + ALIGN)

    packed_mid = lax.all_gather(pack_layer(weight_mid, bias_mid), "gx", axis=0, tiled=True)
    packed_out = lax.all_gather(pack_layer(weight_out, bias_out), "gx", axis=0, tiled=True)

    band_index = jnp.arange(devices, dtype=jnp.int32)
    first_lat = jnp.sum((strip_table[None, :] < band_index[:, None]).astype(jnp.int32), 1)
    end_lat = jnp.sum((strip_table[None, :] <= band_index[:, None]).astype(jnp.int32), 1)
    lo = first_lat * lon_dev
    hi = end_lat * lon_dev
    win = jnp.minimum((lo // ALIGN) * ALIGN, rows - window).astype(jnp.int32)

    columns_bf = fields.astype(jnp.bfloat16)
    west_col = passed_along(columns_bf[-1:], "gx", 1)
    east_col = passed_along(columns_bf[:1], "gx", -1)
    padded = jnp.concatenate([west_col, columns_bf, east_col], 0)
    padded = jnp.pad(padded, ((0, 0), (1, 1), (0, 0)))
    kernel = weight_in.reshape(3, 3, channels, hidden)
    summed = lax.conv_general_dilated(
        padded[None],
        kernel,
        (1, 1),
        "VALID",
        dimension_numbers=("NHWC", "HWIO", "NWHC"),
        preferred_element_type=jnp.float32,
    )[0]
    summed = summed + bias_in
    hidden_one = jax.nn.silu(summed).astype(jnp.bfloat16).reshape(rows, hidden)

    hidden_two = band_layer(hidden_one, packed_mid, lo, hi, win, window, True, jnp.bfloat16)
    tendency = band_layer(hidden_two, packed_out, lo, hi, win, window, False, jnp.float32)
    tendency = tendency.reshape(lat_rows, lon_dev, channels).transpose(1, 0, 2)

    speeds = widened(courant.reshape(lon_dev, lat_rows, levels), field_count)
    switch_one = widened(switches[0].reshape(lon_dev, lat_rows, levels).astype(jnp.float32), field_count)
    switch_two = widened(switches[1].reshape(lon_dev, lat_rows, levels).astype(jnp.float32), field_count)
    ahead_col = east_col.astype(jnp.float32)
    section_one = fields - flux_change(fields, ahead_col, speeds, switch_one)
    ahead_two = passed_along(section_one[:1].astype(jnp.bfloat16), "gx", -1).astype(jnp.float32)
    section_two = section_one - flux_change(section_one, ahead_two, speeds, switch_two)
    moved = 0.5 * fields + 0.5 * section_two
    return moved + tendency


def solution(mesh):
    return jax.shard_map(
        on_device,
        mesh=mesh,
        in_specs=(
            P(("group", "gx"), None, None),
            P(("group", "gx"), None),
            P(None, ("group", "gx"), None),
            P("group"),
            P(),
            P(),
            P("gx", None, None),
            P("gx", None),
            P("gx", None, None),
            P("gx", None),
        ),
        out_specs=P(("group", "gx"), None, None),
        check_vma=False,
    )
```

```python
import jax
import jax.numpy as jnp
from jax import lax
from jax.experimental import pallas as pl
from jax.experimental.pallas import tpu as pltpu
from jax.sharding import PartitionSpec as P

BIAS_ROWS = 16
ALIGN = 16


def passed_along(array, axis, by):
    length = lax.axis_size(axis)
    return lax.ppermute(array, axis, [(i, (i + by) % length) for i in range(length)])


def split_three(values):
    high = values.astype(jnp.bfloat16)
    rest = values - high.astype(jnp.float32)
    middle = rest.astype(jnp.bfloat16)
    low = (rest - middle.astype(jnp.float32)).astype(jnp.bfloat16)
    return [high, middle, low]


def pack_layer(weight, bias):
    rows = jnp.stack(split_three(bias[0]), 0)
    rows = jnp.pad(rows, ((0, BIAS_ROWS - rows.shape[0]), (0, 0)))
    return jnp.concatenate([weight[0], rows], 0)[None]


def face_flux(left_vals, right_vals, speeds, switch_now):
    damping = switch_now * speeds * speeds + (1.0 - switch_now) * jnp.abs(speeds)
    return 0.5 * speeds * (left_vals + right_vals) - 0.5 * damping * (right_vals - left_vals)


def flux_change(values, right_col, speeds, switch_now):
    right_vals = jnp.concatenate([values[1:], right_col], 0)
    edge_flux = face_flux(values, right_vals, speeds, switch_now)
    left_flux = passed_along(edge_flux[-1:].astype(jnp.bfloat16), "gx", 1).astype(jnp.float32)
    return edge_flux - jnp.concatenate([left_flux, edge_flux[:-1]], 0)


def make_band_kernel(window, depth):
    def kernel(lo_ref, hi_ref, start_ref, h1_ref, moved_ref, w_hbm, out_ref, wbuf, sem):
        out_ref[...] = moved_ref[...]
        bands = w_hbm.shape[0]
        lon = h1_ref.shape[0]
        inner = h1_ref.shape[-1]
        half = inner + BIAS_ROWS

        def fetch(band, slot):
            return pltpu.make_async_copy(w_hbm.at[band], wbuf.at[slot], sem.at[slot])

        for band in range(depth):
            fetch(band, band).start()

        def body(band, carry):
            slot = band % depth
            fetch(band, slot).wait()
            start = pl.multiple_of(start_ref[band], ALIGN)
            block = jnp.concatenate([h1_ref[l, pl.ds(start, window), :] for l in range(lon)], 0)
            weight_mid = wbuf[slot, 0:inner, :]
            parts = wbuf[slot, inner : inner + 3, :].astype(jnp.float32)
            bias_mid = (parts[0:1] + parts[1:2]) + parts[2:3]
            weight_out = wbuf[slot, half : half + inner, :]
            parts = wbuf[slot, half + inner : half + inner + 3, :].astype(jnp.float32)
            bias_out = (parts[0:1] + parts[1:2]) + parts[2:3]
            middle = jnp.dot(block, weight_mid, preferred_element_type=jnp.float32) + bias_mid
            hidden_two = (middle / (1.0 + jnp.exp(-middle))).astype(jnp.bfloat16)
            result = jnp.dot(hidden_two, weight_out, preferred_element_type=jnp.float32) + bias_out
            result = result.astype(jnp.bfloat16).astype(jnp.float32)

            @pl.when(band + depth < bands)
            def _():
                fetch(band + depth, slot).start()

            lats = start + lax.broadcasted_iota(jnp.int32, (window, 1), 0)
            mask = jnp.logical_and(lats >= lo_ref[band], lats < hi_ref[band])
            for l in range(lon):
                current = out_ref[l, pl.ds(start, window), :]
                piece = result[l * window : (l + 1) * window]
                out_ref[l, pl.ds(start, window), :] = jnp.where(mask, current + piece, current)
            return carry

        lax.fori_loop(0, bands, body, 0)

    return kernel


def band_networks(hidden_one, moved, packed, lo, hi, start, window):
    bands = packed.shape[0]
    depth = min(bands, 16)
    smem = pl.BlockSpec(memory_space=pltpu.SMEM)
    vmem = pl.BlockSpec(memory_space=pltpu.VMEM)
    return pl.pallas_call(
        make_band_kernel(window, depth),
        in_specs=[smem, smem, smem, vmem, vmem, pl.BlockSpec(memory_space=pl.ANY)],
        out_specs=vmem,
        out_shape=jax.ShapeDtypeStruct(moved.shape, moved.dtype),
        scratch_shapes=[
            pltpu.VMEM((depth,) + packed.shape[1:], packed.dtype),
            pltpu.SemaphoreType.DMA((depth,)),
        ],
    )(lo, hi, start, hidden_one, moved, packed)


def widened(values, field_count):
    lon, rows, levels = values.shape
    return jnp.broadcast_to(values[:, :, None, :], (lon, rows, field_count, levels)).reshape(
        lon, rows, field_count * levels
    )


def on_device(
    fields,
    courant,
    switches,
    strip_table,
    weight_in,
    bias_in,
    weight_mid,
    bias_mid,
    weight_out,
    bias_out,
):
    lon_dev, lat_rows, channels = fields.shape
    levels = courant.shape[1] // lat_rows
    field_count = channels // levels
    hidden = weight_in.shape[1]
    devices = lax.axis_size("gx")
    capacity = max(2, 2 * lat_rows // devices)
    window = min(lat_rows, -(-(capacity + ALIGN - 1) // ALIGN) * ALIGN)

    packed = jnp.concatenate([pack_layer(weight_mid, bias_mid), pack_layer(weight_out, bias_out)], 1)
    packed = lax.all_gather(packed, "gx", axis=0, tiled=True)

    band_index = jnp.arange(devices, dtype=jnp.int32)
    first_lat = jnp.sum((strip_table[None, :] < band_index[:, None]).astype(jnp.int32), 1)
    end_lat = jnp.sum((strip_table[None, :] <= band_index[:, None]).astype(jnp.int32), 1)
    start = jnp.minimum((first_lat // ALIGN) * ALIGN, lat_rows - window).astype(jnp.int32)

    columns_bf = fields.astype(jnp.bfloat16)
    west_col = passed_along(columns_bf[-1:], "gx", 1)
    east_col = passed_along(columns_bf[:1], "gx", -1)
    padded = jnp.concatenate([west_col, columns_bf, east_col], 0)
    padded = jnp.pad(padded, ((0, 0), (1, 1), (0, 0)))
    kernel = weight_in.reshape(3, 3, channels, hidden)
    summed = lax.conv_general_dilated(
        padded[None],
        kernel,
        (1, 1),
        "VALID",
        dimension_numbers=("NHWC", "HWIO", "NHWC"),
        preferred_element_type=jnp.float32,
    )[0]
    summed = summed + bias_in
    hidden_one = jax.nn.silu(summed).astype(jnp.bfloat16)

    speeds = widened(courant.reshape(lon_dev, lat_rows, levels), field_count)
    switch_one = widened(switches[0].reshape(lon_dev, lat_rows, levels).astype(jnp.float32), field_count)
    switch_two = widened(switches[1].reshape(lon_dev, lat_rows, levels).astype(jnp.float32), field_count)
    ahead_col = east_col.astype(jnp.float32)
    section_one = fields - flux_change(fields, ahead_col, speeds, switch_one)
    ahead_two = passed_along(section_one[:1].astype(jnp.bfloat16), "gx", -1).astype(jnp.float32)
    section_two = section_one - flux_change(section_one, ahead_two, speeds, switch_two)
    moved = 0.5 * fields + 0.5 * section_two
    return band_networks(hidden_one, moved, packed, first_lat, end_lat, start, window)


def solution(mesh):
    return jax.shard_map(
        on_device,
        mesh=mesh,
        in_specs=(
            P(("group", "gx"), None, None),
            P(("group", "gx"), None),
            P(None, ("group", "gx"), None),
            P("group"),
            P(),
            P(),
            P("gx", None, None),
            P("gx", None),
            P("gx", None, None),
            P("gx", None),
        ),
        out_specs=P(("group", "gx"), None, None),
        check_vma=False,
    )
```

```python
import jax
import jax.numpy as jnp
from jax import lax
from jax.experimental import pallas as pl
from jax.experimental.pallas import tpu as pltpu
from jax.sharding import PartitionSpec as P

BIAS_ROWS = 16
ALIGN = 16


def passed_along(array, axis, by):
    length = lax.axis_size(axis)
    return lax.ppermute(array, axis, [(i, (i + by) % length) for i in range(length)])


def split_three(values):
    high = values.astype(jnp.bfloat16)
    rest = values - high.astype(jnp.float32)
    middle = rest.astype(jnp.bfloat16)
    low = (rest - middle.astype(jnp.float32)).astype(jnp.bfloat16)
    return [high, middle, low]


def pack_layer(weight, bias):
    rows = jnp.stack(split_three(bias[0]), 0)
    rows = jnp.pad(rows, ((0, BIAS_ROWS - rows.shape[0]), (0, 0)))
    return jnp.concatenate([weight[0], rows], 0)[None]


def face_flux(left_vals, right_vals, speeds, switch_now):
    damping = switch_now * speeds * speeds + (1.0 - switch_now) * jnp.abs(speeds)
    return 0.5 * speeds * (left_vals + right_vals) - 0.5 * damping * (right_vals - left_vals)


def flux_change(values, right_col, speeds, switch_now):
    right_vals = jnp.concatenate([values[1:], right_col], 0)
    edge_flux = face_flux(values, right_vals, speeds, switch_now)
    left_flux = passed_along(edge_flux[-1:].astype(jnp.bfloat16), "gx", 1).astype(jnp.float32)
    return edge_flux - jnp.concatenate([left_flux, edge_flux[:-1]], 0)


def make_band_kernel(window, depth):
    def kernel(lo_ref, hi_ref, start_ref, h1_ref, moved_ref, w_hbm, out_ref, wbuf, sem):
        out_ref[...] = moved_ref[...]
        bands = w_hbm.shape[0]
        lon = h1_ref.shape[0]
        inner = h1_ref.shape[-1]
        half = inner + BIAS_ROWS

        def fetch(band, slot):
            return pltpu.make_async_copy(w_hbm.at[band], wbuf.at[slot], sem.at[slot])

        for band in range(depth):
            fetch(band, band).start()

        def body(band, carry):
            slot = band % depth
            fetch(band, slot).wait()
            start = pl.multiple_of(start_ref[band], ALIGN)
            block = jnp.concatenate([h1_ref[l, pl.ds(start, window), :] for l in range(lon)], 0)
            weight_mid = wbuf[slot, 0:inner, :]
            parts = wbuf[slot, inner : inner + 3, :].astype(jnp.float32)
            bias_mid = (parts[0:1] + parts[1:2]) + parts[2:3]
            weight_out = wbuf[slot, half : half + inner, :]
            parts = wbuf[slot, half + inner : half + inner + 3, :].astype(jnp.float32)
            bias_out = (parts[0:1] + parts[1:2]) + parts[2:3]
            middle = jnp.dot(block, weight_mid, preferred_element_type=jnp.float32) + bias_mid
            hidden_two = (middle / (1.0 + jnp.exp(-middle))).astype(jnp.bfloat16)
            result = jnp.dot(hidden_two, weight_out, preferred_element_type=jnp.float32) + bias_out
            result = result.astype(jnp.bfloat16).astype(jnp.float32)

            @pl.when(band + depth < bands)
            def _():
                fetch(band + depth, slot).start()

            lats = start + lax.broadcasted_iota(jnp.int32, (window, 1), 0)
            mask = jnp.logical_and(lats >= lo_ref[band], lats < hi_ref[band])
            for l in range(lon):
                current = out_ref[l, pl.ds(start, window), :]
                piece = result[l * window : (l + 1) * window]
                out_ref[l, pl.ds(start, window), :] = jnp.where(mask, current + piece, current)
            return carry

        lax.fori_loop(0, bands, body, 0, unroll=True if bands <= 16 else 4)

    return kernel


def band_networks(hidden_one, moved, packed, lo, hi, start, window):
    bands = packed.shape[0]
    depth = min(bands, 16)
    smem = pl.BlockSpec(memory_space=pltpu.SMEM)
    vmem = pl.BlockSpec(memory_space=pltpu.VMEM)
    return pl.pallas_call(
        make_band_kernel(window, depth),
        in_specs=[smem, smem, smem, vmem, vmem, pl.BlockSpec(memory_space=pl.ANY)],
        out_specs=vmem,
        out_shape=jax.ShapeDtypeStruct(moved.shape, moved.dtype),
        scratch_shapes=[
            pltpu.VMEM((depth,) + packed.shape[1:], packed.dtype),
            pltpu.SemaphoreType.DMA((depth,)),
        ],
    )(lo, hi, start, hidden_one, moved, packed)


def widened(values, field_count):
    lon, rows, levels = values.shape
    return jnp.broadcast_to(values[:, :, None, :], (lon, rows, field_count, levels)).reshape(
        lon, rows, field_count * levels
    )


def on_device(
    fields,
    courant,
    switches,
    strip_table,
    weight_in,
    bias_in,
    weight_mid,
    bias_mid,
    weight_out,
    bias_out,
):
    lon_dev, lat_rows, channels = fields.shape
    levels = courant.shape[1] // lat_rows
    field_count = channels // levels
    hidden = weight_in.shape[1]
    devices = lax.axis_size("gx")
    capacity = max(2, 2 * lat_rows // devices)
    window = min(lat_rows, -(-(capacity + ALIGN - 1) // ALIGN) * ALIGN)

    packed = jnp.concatenate([pack_layer(weight_mid, bias_mid), pack_layer(weight_out, bias_out)], 1)
    packed = lax.all_gather(packed, "gx", axis=0, tiled=True)

    band_index = jnp.arange(devices, dtype=jnp.int32)
    first_lat = jnp.sum((strip_table[None, :] < band_index[:, None]).astype(jnp.int32), 1)
    end_lat = jnp.sum((strip_table[None, :] <= band_index[:, None]).astype(jnp.int32), 1)
    start = jnp.minimum((first_lat // ALIGN) * ALIGN, lat_rows - window).astype(jnp.int32)

    columns_bf = fields.astype(jnp.bfloat16)
    west_col = passed_along(columns_bf[-1:], "gx", 1)
    east_col = passed_along(columns_bf[:1], "gx", -1)
    padded = jnp.concatenate([west_col, columns_bf, east_col], 0)
    padded = jnp.pad(padded, ((0, 0), (1, 1), (0, 0)))
    kernel = weight_in.reshape(3, 3, channels, hidden)
    summed = lax.conv_general_dilated(
        padded[None],
        kernel,
        (1, 1),
        "VALID",
        dimension_numbers=("NHWC", "HWIO", "NHWC"),
        preferred_element_type=jnp.float32,
    )[0]
    summed = summed + bias_in
    hidden_one = jax.nn.silu(summed).astype(jnp.bfloat16)

    speeds = widened(courant.reshape(lon_dev, lat_rows, levels), field_count)
    switch_one = widened(switches[0].reshape(lon_dev, lat_rows, levels).astype(jnp.float32), field_count)
    switch_two = widened(switches[1].reshape(lon_dev, lat_rows, levels).astype(jnp.float32), field_count)
    ahead_col = east_col.astype(jnp.float32)
    section_one = fields - flux_change(fields, ahead_col, speeds, switch_one)
    ahead_two = passed_along(section_one[:1].astype(jnp.bfloat16), "gx", -1).astype(jnp.float32)
    section_two = section_one - flux_change(section_one, ahead_two, speeds, switch_two)
    moved = 0.5 * fields + 0.5 * section_two
    return band_networks(hidden_one, moved, packed, first_lat, end_lat, start, window)


def solution(mesh):
    return jax.shard_map(
        on_device,
        mesh=mesh,
        in_specs=(
            P(("group", "gx"), None, None),
            P(("group", "gx"), None),
            P(None, ("group", "gx"), None),
            P("group"),
            P(),
            P(),
            P("gx", None, None),
            P("gx", None),
            P("gx", None, None),
            P("gx", None),
        ),
        out_specs=P(("group", "gx"), None, None),
        check_vma=False,
    )
```

```python
import jax
import jax.numpy as jnp
from jax import lax
from jax.experimental import pallas as pl
from jax.experimental.pallas import tpu as pltpu
from jax.sharding import PartitionSpec as P

BIAS_ROWS = 16
ALIGN = 16


def passed_along(array, axis, by):
    length = lax.axis_size(axis)
    return lax.ppermute(array, axis, [(i, (i + by) % length) for i in range(length)])


def split_three(values):
    high = values.astype(jnp.bfloat16)
    rest = values - high.astype(jnp.float32)
    middle = rest.astype(jnp.bfloat16)
    low = (rest - middle.astype(jnp.float32)).astype(jnp.bfloat16)
    return [high, middle, low]


def pack_layer(weight, bias):
    rows = jnp.stack(split_three(bias[0]), 0)
    rows = jnp.pad(rows, ((0, BIAS_ROWS - rows.shape[0]), (0, 0)))
    return jnp.concatenate([weight[0], rows], 0)[None]


def face_flux(left_vals, right_vals, speeds, switch_now):
    damping = switch_now * speeds * speeds + (1.0 - switch_now) * jnp.abs(speeds)
    return 0.5 * speeds * (left_vals + right_vals) - 0.5 * damping * (right_vals - left_vals)


def flux_change(values, right_col, speeds, switch_now):
    right_vals = jnp.concatenate([values[1:], right_col], 0)
    edge_flux = face_flux(values, right_vals, speeds, switch_now)
    left_flux = passed_along(edge_flux[-1:].astype(jnp.bfloat16), "gx", 1).astype(jnp.float32)
    return edge_flux - jnp.concatenate([left_flux, edge_flux[:-1]], 0)


def make_band_kernel(window, depth):
    def kernel(lo_ref, hi_ref, start_ref, me_ref, h1_ref, moved_ref, same_hbm, other_hbm, out_ref, wbuf, sem):
        out_ref[...] = moved_ref[...]
        bands = 2 * same_hbm.shape[0]
        parity = me_ref[0] % 2
        lon = h1_ref.shape[0]
        inner = h1_ref.shape[-1]
        half = inner + BIAS_ROWS

        def fetch(band, slot):
            return pltpu.make_async_copy(same_hbm.at[band // 2], wbuf.at[slot], sem.at[slot])

        def begin(band, slot):
            mine = band % 2 == parity

            @pl.when(mine)
            def _():
                fetch(band, slot).start()

            @pl.when(jnp.logical_not(mine))
            def _():
                pltpu.make_async_copy(other_hbm.at[band // 2], wbuf.at[slot], sem.at[slot]).start()

        for band in range(depth):
            begin(band, band)

        def body(band, carry):
            slot = band % depth
            fetch(band, slot).wait()
            start = pl.multiple_of(start_ref[band], ALIGN)
            block = jnp.concatenate([h1_ref[l, pl.ds(start, window), :] for l in range(lon)], 0)
            weight_mid = wbuf[slot, 0:inner, :]
            parts = wbuf[slot, inner : inner + 3, :].astype(jnp.float32)
            bias_mid = (parts[0:1] + parts[1:2]) + parts[2:3]
            weight_out = wbuf[slot, half : half + inner, :]
            parts = wbuf[slot, half + inner : half + inner + 3, :].astype(jnp.float32)
            bias_out = (parts[0:1] + parts[1:2]) + parts[2:3]
            middle = jnp.dot(block, weight_mid, preferred_element_type=jnp.float32) + bias_mid
            hidden_two = (middle / (1.0 + jnp.exp(-middle))).astype(jnp.bfloat16)
            result = jnp.dot(hidden_two, weight_out, preferred_element_type=jnp.float32) + bias_out
            result = result.astype(jnp.bfloat16).astype(jnp.float32)

            @pl.when(band + depth < bands)
            def _():
                begin(band + depth, slot)

            lats = start + lax.broadcasted_iota(jnp.int32, (window, 1), 0)
            mask = jnp.logical_and(lats >= lo_ref[band], lats < hi_ref[band])
            for l in range(lon):
                current = out_ref[l, pl.ds(start, window), :]
                piece = result[l * window : (l + 1) * window]
                out_ref[l, pl.ds(start, window), :] = jnp.where(mask, current + piece, current)
            return carry

        lax.fori_loop(0, bands, body, 0, unroll=True if bands <= 16 else 4)

    return kernel


def band_networks(hidden_one, moved, same, other, lo, hi, start, window):
    bands = 2 * same.shape[0]
    depth = min(bands, 16)
    smem = pl.BlockSpec(memory_space=pltpu.SMEM)
    vmem = pl.BlockSpec(memory_space=pltpu.VMEM)
    return pl.pallas_call(
        make_band_kernel(window, depth),
        in_specs=[smem, smem, smem, smem, vmem, vmem, pl.BlockSpec(memory_space=pl.ANY), pl.BlockSpec(memory_space=pl.ANY)],
        out_specs=vmem,
        out_shape=jax.ShapeDtypeStruct(moved.shape, moved.dtype),
        scratch_shapes=[
            pltpu.VMEM((depth,) + same.shape[1:], same.dtype),
            pltpu.SemaphoreType.DMA((depth,)),
        ],
    )(lo, hi, start, lax.axis_index("gx").reshape(1).astype(jnp.int32), hidden_one, moved, same, other)


def widened(values, field_count):
    lon, rows, levels = values.shape
    return jnp.broadcast_to(values[:, :, None, :], (lon, rows, field_count, levels)).reshape(
        lon, rows, field_count * levels
    )


def on_device(
    fields,
    courant,
    switches,
    strip_table,
    weight_in,
    bias_in,
    weight_mid,
    bias_mid,
    weight_out,
    bias_out,
):
    lon_dev, lat_rows, channels = fields.shape
    levels = courant.shape[1] // lat_rows
    field_count = channels // levels
    hidden = weight_in.shape[1]
    devices = lax.axis_size("gx")
    capacity = max(2, 2 * lat_rows // devices)
    window = min(lat_rows, -(-(capacity + ALIGN - 1) // ALIGN) * ALIGN)

    packed = jnp.concatenate([pack_layer(weight_mid, bias_mid), pack_layer(weight_out, bias_out)], 1)
    parity_groups = [list(range(p, devices, 2)) for p in range(2)]
    same = lax.all_gather(packed, "gx", axis=0, tiled=True, axis_index_groups=parity_groups)
    other = lax.ppermute(same, "gx", [(i, i ^ 1) for i in range(devices)])

    band_index = jnp.arange(devices, dtype=jnp.int32)
    first_lat = jnp.sum((strip_table[None, :] < band_index[:, None]).astype(jnp.int32), 1)
    end_lat = jnp.sum((strip_table[None, :] <= band_index[:, None]).astype(jnp.int32), 1)
    start = jnp.minimum((first_lat // ALIGN) * ALIGN, lat_rows - window).astype(jnp.int32)

    columns_bf = fields.astype(jnp.bfloat16)
    west_col = passed_along(columns_bf[-1:], "gx", 1)
    east_col = passed_along(columns_bf[:1], "gx", -1)
    padded = jnp.concatenate([west_col, columns_bf, east_col], 0)
    padded = jnp.pad(padded, ((0, 0), (1, 1), (0, 0)))
    kernel = weight_in.reshape(3, 3, channels, hidden)
    summed = lax.conv_general_dilated(
        padded[None],
        kernel,
        (1, 1),
        "VALID",
        dimension_numbers=("NHWC", "HWIO", "NHWC"),
        preferred_element_type=jnp.float32,
    )[0]
    summed = summed + bias_in
    hidden_one = jax.nn.silu(summed).astype(jnp.bfloat16)

    speeds = widened(courant.reshape(lon_dev, lat_rows, levels), field_count)
    switch_one = widened(switches[0].reshape(lon_dev, lat_rows, levels).astype(jnp.float32), field_count)
    switch_two = widened(switches[1].reshape(lon_dev, lat_rows, levels).astype(jnp.float32), field_count)
    ahead_col = east_col.astype(jnp.float32)
    section_one = fields - flux_change(fields, ahead_col, speeds, switch_one)
    ahead_two = passed_along(section_one[:1].astype(jnp.bfloat16), "gx", -1).astype(jnp.float32)
    section_two = section_one - flux_change(section_one, ahead_two, speeds, switch_two)
    moved = 0.5 * fields + 0.5 * section_two
    return band_networks(hidden_one, moved, same, other, first_lat, end_lat, start, window)


def solution(mesh):
    return jax.shard_map(
        on_device,
        mesh=mesh,
        in_specs=(
            P(("group", "gx"), None, None),
            P(("group", "gx"), None),
            P(None, ("group", "gx"), None),
            P("group"),
            P(),
            P(),
            P("gx", None, None),
            P("gx", None),
            P("gx", None, None),
            P("gx", None),
        ),
        out_specs=P(("group", "gx"), None, None),
        check_vma=False,
    )
```

```python
import jax
import jax.numpy as jnp
from jax import lax
from jax.experimental import pallas as pl
from jax.experimental.pallas import tpu as pltpu
from jax.sharding import PartitionSpec as P

BIAS_ROWS = 16
ALIGN = 16


def passed_along(array, axis, by):
    length = lax.axis_size(axis)
    return lax.ppermute(array, axis, [(i, (i + by) % length) for i in range(length)])


def split_three(values):
    high = values.astype(jnp.bfloat16)
    rest = values - high.astype(jnp.float32)
    middle = rest.astype(jnp.bfloat16)
    low = (rest - middle.astype(jnp.float32)).astype(jnp.bfloat16)
    return [high, middle, low]


def pack_layer(weight, bias):
    rows = jnp.stack(split_three(bias[0]), 0)
    rows = jnp.pad(rows, ((0, BIAS_ROWS - rows.shape[0]), (0, 0)))
    return jnp.concatenate([weight[0], rows], 0)[None]


def face_flux(left_vals, right_vals, speeds, switch_now):
    damping = switch_now * speeds * speeds + (1.0 - switch_now) * jnp.abs(speeds)
    return 0.5 * speeds * (left_vals + right_vals) - 0.5 * damping * (right_vals - left_vals)


def flux_change(values, right_col, speeds, switch_now):
    right_vals = jnp.concatenate([values[1:], right_col], 0)
    edge_flux = face_flux(values, right_vals, speeds, switch_now)
    left_flux = passed_along(edge_flux[-1:].astype(jnp.bfloat16), "gx", 1).astype(jnp.float32)
    return edge_flux - jnp.concatenate([left_flux, edge_flux[:-1]], 0)


def make_band_kernel(window, depth):
    def kernel(lo_ref, hi_ref, start_ref, h1_ref, moved_ref, w_hbm, out_ref, wbuf, sem):
        out_ref[...] = moved_ref[...]
        bands = w_hbm.shape[0] // 2
        lon = h1_ref.shape[0]
        inner = h1_ref.shape[-1]
        half = inner + BIAS_ROWS

        def fetch(band, slot, part):
            return pltpu.make_async_copy(
                w_hbm.at[band + part * bands], wbuf.at[slot, pl.ds(part * half, half)], sem.at[slot, part]
            )

        def begin(band, slot):
            fetch(band, slot, 0).start()
            fetch(band, slot, 1).start()

        for band in range(depth):
            begin(band, band)

        def body(band, carry):
            slot = band % depth
            fetch(band, slot, 0).wait()
            fetch(band, slot, 1).wait()
            start = pl.multiple_of(start_ref[band], ALIGN)
            block = jnp.concatenate([h1_ref[l, pl.ds(start, window), :] for l in range(lon)], 0)
            weight_mid = wbuf[slot, 0:inner, :]
            parts = wbuf[slot, inner : inner + 3, :].astype(jnp.float32)
            bias_mid = (parts[0:1] + parts[1:2]) + parts[2:3]
            weight_out = wbuf[slot, half : half + inner, :]
            parts = wbuf[slot, half + inner : half + inner + 3, :].astype(jnp.float32)
            bias_out = (parts[0:1] + parts[1:2]) + parts[2:3]
            middle = jnp.dot(block, weight_mid, preferred_element_type=jnp.float32) + bias_mid
            hidden_two = (middle / (1.0 + jnp.exp(-middle))).astype(jnp.bfloat16)
            result = jnp.dot(hidden_two, weight_out, preferred_element_type=jnp.float32) + bias_out
            result = result.astype(jnp.bfloat16).astype(jnp.float32)

            @pl.when(band + depth < bands)
            def _():
                begin(band + depth, slot)

            lats = start + lax.broadcasted_iota(jnp.int32, (window, 1), 0)
            mask = jnp.logical_and(lats >= lo_ref[band], lats < hi_ref[band])
            for l in range(lon):
                current = out_ref[l, pl.ds(start, window), :]
                piece = result[l * window : (l + 1) * window]
                out_ref[l, pl.ds(start, window), :] = jnp.where(mask, current + piece, current)
            return carry

        lax.fori_loop(0, bands, body, 0, unroll=True if bands <= 16 else 4)

    return kernel


def band_networks(hidden_one, moved, packed, lo, hi, start, window):
    bands = packed.shape[0] // 2
    depth = min(bands, 16)
    smem = pl.BlockSpec(memory_space=pltpu.SMEM)
    vmem = pl.BlockSpec(memory_space=pltpu.VMEM)
    return pl.pallas_call(
        make_band_kernel(window, depth),
        in_specs=[smem, smem, smem, vmem, vmem, pl.BlockSpec(memory_space=pl.ANY)],
        out_specs=vmem,
        out_shape=jax.ShapeDtypeStruct(moved.shape, moved.dtype),
        scratch_shapes=[
            pltpu.VMEM((depth, 2 * packed.shape[1], packed.shape[2]), packed.dtype),
            pltpu.SemaphoreType.DMA((depth, 2)),
        ],
    )(lo, hi, start, hidden_one, moved, packed)


def widened(values, field_count):
    lon, rows, levels = values.shape
    return jnp.broadcast_to(values[:, :, None, :], (lon, rows, field_count, levels)).reshape(
        lon, rows, field_count * levels
    )


def on_device(
    fields,
    courant,
    switches,
    strip_table,
    weight_in,
    bias_in,
    weight_mid,
    bias_mid,
    weight_out,
    bias_out,
):
    lon_dev, lat_rows, channels = fields.shape
    levels = courant.shape[1] // lat_rows
    field_count = channels // levels
    hidden = weight_in.shape[1]
    devices = lax.axis_size("gx")
    capacity = max(2, 2 * lat_rows // devices)
    window = min(lat_rows, -(-(capacity + ALIGN - 1) // ALIGN) * ALIGN)

    packed = jnp.concatenate([pack_layer(weight_mid, bias_mid), pack_layer(weight_out, bias_out)], 1)
    half_rows = packed.shape[1] // 2
    share = lax.dynamic_slice_in_dim(packed, lax.axis_index("group") * half_rows, half_rows, 1)
    packed = lax.all_gather(share, ("group", "gx"), axis=0, tiled=True)

    band_index = jnp.arange(devices, dtype=jnp.int32)
    first_lat = jnp.sum((strip_table[None, :] < band_index[:, None]).astype(jnp.int32), 1)
    end_lat = jnp.sum((strip_table[None, :] <= band_index[:, None]).astype(jnp.int32), 1)
    start = jnp.minimum((first_lat // ALIGN) * ALIGN, lat_rows - window).astype(jnp.int32)

    columns_bf = fields.astype(jnp.bfloat16)
    west_col = passed_along(columns_bf[-1:], "gx", 1)
    east_col = passed_along(columns_bf[:1], "gx", -1)
    padded = jnp.concatenate([west_col, columns_bf, east_col], 0)
    padded = jnp.pad(padded, ((0, 0), (1, 1), (0, 0)))
    kernel = weight_in.reshape(3, 3, channels, hidden)
    summed = lax.conv_general_dilated(
        padded[None],
        kernel,
        (1, 1),
        "VALID",
        dimension_numbers=("NHWC", "HWIO", "NHWC"),
        preferred_element_type=jnp.float32,
    )[0]
    summed = summed + bias_in
    hidden_one = jax.nn.silu(summed).astype(jnp.bfloat16)

    speeds = widened(courant.reshape(lon_dev, lat_rows, levels), field_count)
    switch_one = widened(switches[0].reshape(lon_dev, lat_rows, levels).astype(jnp.float32), field_count)
    switch_two = widened(switches[1].reshape(lon_dev, lat_rows, levels).astype(jnp.float32), field_count)
    ahead_col = east_col.astype(jnp.float32)
    section_one = fields - flux_change(fields, ahead_col, speeds, switch_one)
    ahead_two = passed_along(section_one[:1].astype(jnp.bfloat16), "gx", -1).astype(jnp.float32)
    section_two = section_one - flux_change(section_one, ahead_two, speeds, switch_two)
    moved = 0.5 * fields + 0.5 * section_two
    return band_networks(hidden_one, moved, packed, first_lat, end_lat, start, window)


def solution(mesh):
    return jax.shard_map(
        on_device,
        mesh=mesh,
        in_specs=(
            P(("group", "gx"), None, None),
            P(("group", "gx"), None),
            P(None, ("group", "gx"), None),
            P("group"),
            P(),
            P(),
            P("gx", None, None),
            P("gx", None),
            P("gx", None, None),
            P("gx", None),
        ),
        out_specs=P(("group", "gx"), None, None),
        check_vma=False,
    )
```

```python
import jax
import jax.numpy as jnp
from jax import lax
from jax.experimental import pallas as pl
from jax.experimental.pallas import tpu as pltpu
from jax.sharding import PartitionSpec as P

BIAS_ROWS = 16
ALIGN = 16
RESIDENT_BYTES = 8 * 1024 * 1024


def passed_along(array, axis, by):
    length = lax.axis_size(axis)
    return lax.ppermute(array, axis, [(i, (i + by) % length) for i in range(length)])


def split_three(values):
    high = values.astype(jnp.bfloat16)
    rest = values - high.astype(jnp.float32)
    middle = rest.astype(jnp.bfloat16)
    low = (rest - middle.astype(jnp.float32)).astype(jnp.bfloat16)
    return [high, middle, low]


def pack_layer(weight, bias):
    rows = jnp.stack(split_three(bias[0]), 0)
    rows = jnp.pad(rows, ((0, BIAS_ROWS - rows.shape[0]), (0, 0)))
    return jnp.concatenate([weight[0], rows], 0)[None]


def face_flux(left_vals, right_vals, speeds, switch_now):
    damping = switch_now * speeds * speeds + (1.0 - switch_now) * jnp.abs(speeds)
    return 0.5 * speeds * (left_vals + right_vals) - 0.5 * damping * (right_vals - left_vals)


def flux_change(values, right_col, speeds, switch_now):
    right_vals = jnp.concatenate([values[1:], right_col], 0)
    edge_flux = face_flux(values, right_vals, speeds, switch_now)
    left_flux = passed_along(edge_flux[-1:].astype(jnp.bfloat16), "gx", 1).astype(jnp.float32)
    return edge_flux - jnp.concatenate([left_flux, edge_flux[:-1]], 0)


def make_band_kernel(window, depth, resident):
    def kernel(lo_ref, hi_ref, start_ref, h1_ref, moved_ref, w_hbm, out_ref, *scratch):
        out_ref[...] = moved_ref[...]
        bands = w_hbm.shape[0]
        lon = h1_ref.shape[0]
        inner = h1_ref.shape[-1]
        half = inner + BIAS_ROWS
        if resident:
            wbuf = w_hbm
        else:
            wbuf, sem = scratch

            def fetch(band, slot):
                return pltpu.make_async_copy(w_hbm.at[band], wbuf.at[slot], sem.at[slot])

            for band in range(depth):
                fetch(band, band).start()

        def body(band, carry):
            if resident:
                slot = band
            else:
                slot = band % depth
                fetch(band, slot).wait()
            start = pl.multiple_of(start_ref[band], ALIGN)
            block = jnp.concatenate([h1_ref[l, pl.ds(start, window), :] for l in range(lon)], 0)
            weight_mid = wbuf[slot, 0:inner, :]
            parts = wbuf[slot, inner : inner + 3, :].astype(jnp.float32)
            bias_mid = (parts[0:1] + parts[1:2]) + parts[2:3]
            weight_out = wbuf[slot, half : half + inner, :]
            parts = wbuf[slot, half + inner : half + inner + 3, :].astype(jnp.float32)
            bias_out = (parts[0:1] + parts[1:2]) + parts[2:3]
            middle = jnp.dot(block, weight_mid, preferred_element_type=jnp.float32) + bias_mid
            hidden_two = (middle / (1.0 + jnp.exp(-middle))).astype(jnp.bfloat16)
            result = jnp.dot(hidden_two, weight_out, preferred_element_type=jnp.float32) + bias_out
            result = result.astype(jnp.bfloat16).astype(jnp.float32)

            if not resident:

                @pl.when(band + depth < bands)
                def _():
                    fetch(band + depth, slot).start()

            lats = start + lax.broadcasted_iota(jnp.int32, (window, 1), 0)
            mask = jnp.logical_and(lats >= lo_ref[band], lats < hi_ref[band])
            for l in range(lon):
                current = out_ref[l, pl.ds(start, window), :]
                piece = result[l * window : (l + 1) * window]
                out_ref[l, pl.ds(start, window), :] = jnp.where(mask, current + piece, current)
            return carry

        lax.fori_loop(0, bands, body, 0, unroll=True if bands <= 16 else 4)

    return kernel


def band_networks(hidden_one, moved, packed, lo, hi, start, window):
    bands = packed.shape[0]
    depth = min(bands, 16)
    resident = packed.size * packed.dtype.itemsize <= RESIDENT_BYTES
    smem = pl.BlockSpec(memory_space=pltpu.SMEM)
    vmem = pl.BlockSpec(memory_space=pltpu.VMEM)
    if resident:
        weights_spec, scratch = vmem, []
    else:
        weights_spec = pl.BlockSpec(memory_space=pl.ANY)
        scratch = [
            pltpu.VMEM((depth,) + packed.shape[1:], packed.dtype),
            pltpu.SemaphoreType.DMA((depth,)),
        ]
    return pl.pallas_call(
        make_band_kernel(window, depth, resident),
        in_specs=[smem, smem, smem, vmem, vmem, weights_spec],
        out_specs=vmem,
        out_shape=jax.ShapeDtypeStruct(moved.shape, moved.dtype),
        scratch_shapes=scratch,
    )(lo, hi, start, hidden_one, moved, packed)


def widened(values, field_count):
    lon, rows, levels = values.shape
    return jnp.broadcast_to(values[:, :, None, :], (lon, rows, field_count, levels)).reshape(
        lon, rows, field_count * levels
    )


def on_device(
    fields,
    courant,
    switches,
    strip_table,
    weight_in,
    bias_in,
    weight_mid,
    bias_mid,
    weight_out,
    bias_out,
):
    lon_dev, lat_rows, channels = fields.shape
    levels = courant.shape[1] // lat_rows
    field_count = channels // levels
    hidden = weight_in.shape[1]
    devices = lax.axis_size("gx")
    capacity = max(2, 2 * lat_rows // devices)
    window = min(lat_rows, -(-(capacity + ALIGN - 1) // ALIGN) * ALIGN)

    packed = jnp.concatenate([pack_layer(weight_mid, bias_mid), pack_layer(weight_out, bias_out)], 1)
    packed = lax.all_gather(packed, "gx", axis=0, tiled=True)

    band_index = jnp.arange(devices, dtype=jnp.int32)
    first_lat = jnp.sum((strip_table[None, :] < band_index[:, None]).astype(jnp.int32), 1)
    end_lat = jnp.sum((strip_table[None, :] <= band_index[:, None]).astype(jnp.int32), 1)
    start = jnp.minimum((first_lat // ALIGN) * ALIGN, lat_rows - window).astype(jnp.int32)

    columns_bf = fields.astype(jnp.bfloat16)
    west_col = passed_along(columns_bf[-1:], "gx", 1)
    east_col = passed_along(columns_bf[:1], "gx", -1)
    padded = jnp.concatenate([west_col, columns_bf, east_col], 0)
    padded = jnp.pad(padded, ((0, 0), (1, 1), (0, 0)))
    kernel = weight_in.reshape(3, 3, channels, hidden)
    summed = lax.conv_general_dilated(
        padded[None],
        kernel,
        (1, 1),
        "VALID",
        dimension_numbers=("NHWC", "HWIO", "NHWC"),
        preferred_element_type=jnp.float32,
    )[0]
    summed = summed + bias_in
    hidden_one = jax.nn.silu(summed).astype(jnp.bfloat16)

    speeds = widened(courant.reshape(lon_dev, lat_rows, levels), field_count)
    switch_one = widened(switches[0].reshape(lon_dev, lat_rows, levels).astype(jnp.float32), field_count)
    switch_two = widened(switches[1].reshape(lon_dev, lat_rows, levels).astype(jnp.float32), field_count)
    ahead_col = east_col.astype(jnp.float32)
    section_one = fields - flux_change(fields, ahead_col, speeds, switch_one)
    ahead_two = passed_along(section_one[:1].astype(jnp.bfloat16), "gx", -1).astype(jnp.float32)
    section_two = section_one - flux_change(section_one, ahead_two, speeds, switch_two)
    moved = 0.5 * fields + 0.5 * section_two
    return band_networks(hidden_one, moved, packed, first_lat, end_lat, start, window)


def solution(mesh):
    return jax.shard_map(
        on_device,
        mesh=mesh,
        in_specs=(
            P(("group", "gx"), None, None),
            P(("group", "gx"), None),
            P(None, ("group", "gx"), None),
            P("group"),
            P(),
            P(),
            P("gx", None, None),
            P("gx", None),
            P("gx", None, None),
            P("gx", None),
        ),
        out_specs=P(("group", "gx"), None, None),
        check_vma=False,
    )
```

```python
import jax
import jax.numpy as jnp
from jax import lax
from jax.experimental import pallas as pl
from jax.experimental.pallas import tpu as pltpu
from jax.sharding import PartitionSpec as P

BIAS_ROWS = 16
ALIGN = 16
RESIDENT_BYTES = 8 * 1024 * 1024


def passed_along(array, axis, by):
    length = lax.axis_size(axis)
    return lax.ppermute(array, axis, [(i, (i + by) % length) for i in range(length)])


def split_three(values):
    high = values.astype(jnp.bfloat16)
    rest = values - high.astype(jnp.float32)
    middle = rest.astype(jnp.bfloat16)
    low = (rest - middle.astype(jnp.float32)).astype(jnp.bfloat16)
    return [high, middle, low]


def pack_layer(weight, bias):
    rows = jnp.stack(split_three(bias[0]), 0)
    rows = jnp.pad(rows, ((0, BIAS_ROWS - rows.shape[0]), (0, 0)))
    return jnp.concatenate([weight[0], rows], 0)[None]


def bias_rows(bias_ref):
    lanes = bias_ref.shape[-1]
    values = jnp.broadcast_to(bias_ref[...].astype(jnp.float32), (BIAS_ROWS, lanes))
    high = values.astype(jnp.bfloat16).astype(jnp.float32)
    rest = values - high
    middle = rest.astype(jnp.bfloat16).astype(jnp.float32)
    low = (rest - middle).astype(jnp.bfloat16).astype(jnp.float32)
    row = lax.broadcasted_iota(jnp.int32, (BIAS_ROWS, lanes), 0)
    rows = jnp.where(row == 0, high, jnp.where(row == 1, middle, jnp.where(row == 2, low, 0.0)))
    return rows.astype(jnp.bfloat16)


def pack_kernel(wm_ref, bm_ref, wo_ref, bo_ref, out_ref):
    inner = wm_ref.shape[1]
    half = inner + BIAS_ROWS
    out_ref[0, 0:inner, :] = wm_ref[0]
    out_ref[0, inner:half, :] = bias_rows(bm_ref)
    out_ref[0, half : half + inner, :] = wo_ref[0]
    out_ref[0, half + inner : 2 * half, :] = bias_rows(bo_ref)


def pack_bands(weight_mid, bias_mid, weight_out, bias_out):
    inner, lanes = weight_mid.shape[1:]
    return pl.pallas_call(
        pack_kernel,
        out_shape=jax.ShapeDtypeStruct((1, 2 * (inner + BIAS_ROWS), lanes), weight_mid.dtype),
    )(weight_mid, bias_mid, weight_out, bias_out)


def face_flux(left_vals, right_vals, speeds, switch_now):
    damping = switch_now * speeds * speeds + (1.0 - switch_now) * jnp.abs(speeds)
    return 0.5 * speeds * (left_vals + right_vals) - 0.5 * damping * (right_vals - left_vals)


def flux_change(values, right_col, speeds, switch_now):
    right_vals = jnp.concatenate([values[1:], right_col], 0)
    edge_flux = face_flux(values, right_vals, speeds, switch_now)
    left_flux = passed_along(edge_flux[-1:].astype(jnp.bfloat16), "gx", 1).astype(jnp.float32)
    return edge_flux - jnp.concatenate([left_flux, edge_flux[:-1]], 0)


def make_band_kernel(window, depth, resident):
    def kernel(lo_ref, hi_ref, start_ref, h1_ref, moved_ref, w_hbm, out_ref, *scratch):
        out_ref[...] = moved_ref[...]
        bands = w_hbm.shape[0]
        lon = h1_ref.shape[0]
        inner = h1_ref.shape[-1]
        half = inner + BIAS_ROWS
        if resident:
            wbuf = w_hbm
        else:
            wbuf, sem = scratch

            def fetch(band, slot):
                return pltpu.make_async_copy(w_hbm.at[band], wbuf.at[slot], sem.at[slot])

            for band in range(depth):
                fetch(band, band).start()

        def body(band, carry):
            if resident:
                slot = band
            else:
                slot = band % depth
                fetch(band, slot).wait()
            start = pl.multiple_of(start_ref[band], ALIGN)
            block = jnp.concatenate([h1_ref[l, pl.ds(start, window), :] for l in range(lon)], 0)
            weight_mid = wbuf[slot, 0:inner, :]
            parts = wbuf[slot, inner : inner + 3, :].astype(jnp.float32)
            bias_mid = (parts[0:1] + parts[1:2]) + parts[2:3]
            weight_out = wbuf[slot, half : half + inner, :]
            parts = wbuf[slot, half + inner : half + inner + 3, :].astype(jnp.float32)
            bias_out = (parts[0:1] + parts[1:2]) + parts[2:3]
            middle = jnp.dot(block, weight_mid, preferred_element_type=jnp.float32) + bias_mid
            hidden_two = (middle / (1.0 + jnp.exp(-middle))).astype(jnp.bfloat16)
            result = jnp.dot(hidden_two, weight_out, preferred_element_type=jnp.float32) + bias_out
            result = result.astype(jnp.bfloat16).astype(jnp.float32)

            if not resident:

                @pl.when(band + depth < bands)
                def _():
                    fetch(band + depth, slot).start()

            lats = start + lax.broadcasted_iota(jnp.int32, (window, 1), 0)
            mask = jnp.logical_and(lats >= lo_ref[band], lats < hi_ref[band])
            for l in range(lon):
                current = out_ref[l, pl.ds(start, window), :]
                piece = result[l * window : (l + 1) * window]
                out_ref[l, pl.ds(start, window), :] = jnp.where(mask, current + piece, current)
            return carry

        lax.fori_loop(0, bands, body, 0, unroll=True if bands <= 16 else 4)

    return kernel


def band_networks(hidden_one, moved, packed, lo, hi, start, window):
    bands = packed.shape[0]
    depth = min(bands, 16)
    resident = packed.size * packed.dtype.itemsize <= RESIDENT_BYTES
    smem = pl.BlockSpec(memory_space=pltpu.SMEM)
    vmem = pl.BlockSpec(memory_space=pltpu.VMEM)
    if resident:
        weights_spec, scratch = vmem, []
    else:
        weights_spec = pl.BlockSpec(memory_space=pl.ANY)
        scratch = [
            pltpu.VMEM((depth,) + packed.shape[1:], packed.dtype),
            pltpu.SemaphoreType.DMA((depth,)),
        ]
    return pl.pallas_call(
        make_band_kernel(window, depth, resident),
        in_specs=[smem, smem, smem, vmem, vmem, weights_spec],
        out_specs=vmem,
        out_shape=jax.ShapeDtypeStruct(moved.shape, moved.dtype),
        scratch_shapes=scratch,
    )(lo, hi, start, hidden_one, moved, packed)


def widened(values, field_count):
    lon, rows, levels = values.shape
    return jnp.broadcast_to(values[:, :, None, :], (lon, rows, field_count, levels)).reshape(
        lon, rows, field_count * levels
    )


def on_device(
    fields,
    courant,
    switches,
    strip_table,
    weight_in,
    bias_in,
    weight_mid,
    bias_mid,
    weight_out,
    bias_out,
):
    lon_dev, lat_rows, channels = fields.shape
    levels = courant.shape[1] // lat_rows
    field_count = channels // levels
    hidden = weight_in.shape[1]
    devices = lax.axis_size("gx")
    capacity = max(2, 2 * lat_rows // devices)
    window = min(lat_rows, -(-(capacity + ALIGN - 1) // ALIGN) * ALIGN)

    packed = pack_bands(weight_mid, bias_mid, weight_out, bias_out)
    packed = lax.all_gather(packed, "gx", axis=0, tiled=True)

    band_index = jnp.arange(devices, dtype=jnp.int32)
    first_lat = jnp.sum((strip_table[None, :] < band_index[:, None]).astype(jnp.int32), 1)
    end_lat = jnp.sum((strip_table[None, :] <= band_index[:, None]).astype(jnp.int32), 1)
    start = jnp.minimum((first_lat // ALIGN) * ALIGN, lat_rows - window).astype(jnp.int32)

    columns_bf = fields.astype(jnp.bfloat16)
    west_col = passed_along(columns_bf[-1:], "gx", 1)
    east_col = passed_along(columns_bf[:1], "gx", -1)
    padded = jnp.concatenate([west_col, columns_bf, east_col], 0)
    padded = jnp.pad(padded, ((0, 0), (1, 1), (0, 0)))
    kernel = weight_in.reshape(3, 3, channels, hidden)
    summed = lax.conv_general_dilated(
        padded[None],
        kernel,
        (1, 1),
        "VALID",
        dimension_numbers=("NHWC", "HWIO", "NHWC"),
        preferred_element_type=jnp.float32,
    )[0]
    summed = summed + bias_in
    hidden_one = jax.nn.silu(summed).astype(jnp.bfloat16)

    speeds = widened(courant.reshape(lon_dev, lat_rows, levels), field_count)
    switch_one = widened(switches[0].reshape(lon_dev, lat_rows, levels).astype(jnp.float32), field_count)
    switch_two = widened(switches[1].reshape(lon_dev, lat_rows, levels).astype(jnp.float32), field_count)
    ahead_col = east_col.astype(jnp.float32)
    section_one = fields - flux_change(fields, ahead_col, speeds, switch_one)
    ahead_two = passed_along(section_one[:1].astype(jnp.bfloat16), "gx", -1).astype(jnp.float32)
    section_two = section_one - flux_change(section_one, ahead_two, speeds, switch_two)
    moved = 0.5 * fields + 0.5 * section_two
    return band_networks(hidden_one, moved, packed, first_lat, end_lat, start, window)


def solution(mesh):
    return jax.shard_map(
        on_device,
        mesh=mesh,
        in_specs=(
            P(("group", "gx"), None, None),
            P(("group", "gx"), None),
            P(None, ("group", "gx"), None),
            P("group"),
            P(),
            P(),
            P("gx", None, None),
            P("gx", None),
            P("gx", None, None),
            P("gx", None),
        ),
        out_specs=P(("group", "gx"), None, None),
        check_vma=False,
    )
```

```python
import jax
import jax.numpy as jnp
from jax import lax
from jax.experimental import pallas as pl
from jax.experimental.pallas import tpu as pltpu
from jax.sharding import PartitionSpec as P

BIAS_ROWS = 16
ALIGN = 16
RESIDENT_BYTES = 8 * 1024 * 1024


def passed_along(array, axis, by):
    length = lax.axis_size(axis)
    return lax.ppermute(array, axis, [(i, (i + by) % length) for i in range(length)])


def split_three(values):
    high = values.astype(jnp.bfloat16)
    rest = values - high.astype(jnp.float32)
    middle = rest.astype(jnp.bfloat16)
    low = (rest - middle.astype(jnp.float32)).astype(jnp.bfloat16)
    return [high, middle, low]


def pack_layer(weight, bias):
    rows = jnp.stack(split_three(bias[0]), 0)
    rows = jnp.pad(rows, ((0, BIAS_ROWS - rows.shape[0]), (0, 0)))
    return jnp.concatenate([weight[0], rows], 0)[None]


def split_rows(bias_ref, first, row):
    lanes = bias_ref.shape[-1]
    values = jnp.broadcast_to(bias_ref[...].astype(jnp.float32), (BIAS_ROWS, lanes))
    high = values.astype(jnp.bfloat16).astype(jnp.float32)
    rest = values - high
    middle = rest.astype(jnp.bfloat16).astype(jnp.float32)
    low = (rest - middle).astype(jnp.bfloat16).astype(jnp.float32)
    return jnp.where(row == first, high, jnp.where(row == first + 1, middle, jnp.where(row == first + 2, low, 0.0)))


def pack_kernel(wm_ref, bm_ref, wo_ref, bo_ref, out_ref):
    inner = wm_ref.shape[1]
    lanes = wm_ref.shape[2]
    out_ref[0, 0:inner, :] = wm_ref[0]
    out_ref[0, inner : 2 * inner, :] = wo_ref[0]
    row = lax.broadcasted_iota(jnp.int32, (BIAS_ROWS, lanes), 0)
    rows = split_rows(bm_ref, 0, row) + split_rows(bo_ref, 3, row)
    out_ref[0, 2 * inner : 2 * inner + BIAS_ROWS, :] = rows.astype(jnp.bfloat16)


def pack_bands(weight_mid, bias_mid, weight_out, bias_out):
    inner, lanes = weight_mid.shape[1:]
    return pl.pallas_call(
        pack_kernel,
        out_shape=jax.ShapeDtypeStruct((1, 2 * inner + BIAS_ROWS, lanes), weight_mid.dtype),
    )(weight_mid, bias_mid, weight_out, bias_out)


def face_flux(left_vals, right_vals, speeds, switch_now):
    damping = switch_now * speeds * speeds + (1.0 - switch_now) * jnp.abs(speeds)
    return 0.5 * speeds * (left_vals + right_vals) - 0.5 * damping * (right_vals - left_vals)


def flux_change(values, right_col, speeds, switch_now):
    right_vals = jnp.concatenate([values[1:], right_col], 0)
    edge_flux = face_flux(values, right_vals, speeds, switch_now)
    left_flux = passed_along(edge_flux[-1:].astype(jnp.bfloat16), "gx", 1).astype(jnp.float32)
    return edge_flux - jnp.concatenate([left_flux, edge_flux[:-1]], 0)


def make_band_kernel(window, depth, resident):
    def kernel(lo_ref, hi_ref, start_ref, h1_ref, moved_ref, w_hbm, out_ref, *scratch):
        out_ref[...] = moved_ref[...]
        bands = w_hbm.shape[0]
        lon = h1_ref.shape[0]
        inner = h1_ref.shape[-1]
        if resident:
            wbuf = w_hbm
        else:
            wbuf, sem = scratch

            def fetch(band, slot):
                return pltpu.make_async_copy(w_hbm.at[band], wbuf.at[slot], sem.at[slot])

            for band in range(depth):
                fetch(band, band).start()

        def body(band, carry):
            if resident:
                slot = band
            else:
                slot = band % depth
                fetch(band, slot).wait()
            start = pl.multiple_of(start_ref[band], ALIGN)
            block = jnp.concatenate([h1_ref[l, pl.ds(start, window), :] for l in range(lon)], 0)
            weight_mid = wbuf[slot, 0:inner, :]
            weight_out = wbuf[slot, inner : 2 * inner, :]
            parts = wbuf[slot, 2 * inner : 2 * inner + 8, :].astype(jnp.float32)
            bias_mid = (parts[0:1] + parts[1:2]) + parts[2:3]
            bias_out = (parts[3:4] + parts[4:5]) + parts[5:6]
            middle = jnp.dot(block, weight_mid, preferred_element_type=jnp.float32) + bias_mid
            hidden_two = (middle / (1.0 + jnp.exp(-middle))).astype(jnp.bfloat16)
            result = jnp.dot(hidden_two, weight_out, preferred_element_type=jnp.float32) + bias_out
            result = result.astype(jnp.bfloat16).astype(jnp.float32)

            if not resident:

                @pl.when(band + depth < bands)
                def _():
                    fetch(band + depth, slot).start()

            lats = start + lax.broadcasted_iota(jnp.int32, (window, 1), 0)
            mask = jnp.logical_and(lats >= lo_ref[band], lats < hi_ref[band])
            for l in range(lon):
                current = out_ref[l, pl.ds(start, window), :]
                piece = result[l * window : (l + 1) * window]
                out_ref[l, pl.ds(start, window), :] = jnp.where(mask, current + piece, current)
            return carry

        lax.fori_loop(0, bands, body, 0, unroll=True if bands <= 16 else 4)

    return kernel


def band_networks(hidden_one, moved, packed, lo, hi, start, window):
    bands = packed.shape[0]
    depth = min(bands, 16)
    resident = packed.size * packed.dtype.itemsize <= RESIDENT_BYTES
    smem = pl.BlockSpec(memory_space=pltpu.SMEM)
    vmem = pl.BlockSpec(memory_space=pltpu.VMEM)
    if resident:
        weights_spec, scratch = vmem, []
    else:
        weights_spec = pl.BlockSpec(memory_space=pl.ANY)
        scratch = [
            pltpu.VMEM((depth,) + packed.shape[1:], packed.dtype),
            pltpu.SemaphoreType.DMA((depth,)),
        ]
    return pl.pallas_call(
        make_band_kernel(window, depth, resident),
        in_specs=[smem, smem, smem, vmem, vmem, weights_spec],
        out_specs=vmem,
        out_shape=jax.ShapeDtypeStruct(moved.shape, moved.dtype),
        scratch_shapes=scratch,
    )(lo, hi, start, hidden_one, moved, packed)


def widened(values, field_count):
    lon, rows, levels = values.shape
    return jnp.broadcast_to(values[:, :, None, :], (lon, rows, field_count, levels)).reshape(
        lon, rows, field_count * levels
    )


def on_device(
    fields,
    courant,
    switches,
    strip_table,
    weight_in,
    bias_in,
    weight_mid,
    bias_mid,
    weight_out,
    bias_out,
):
    lon_dev, lat_rows, channels = fields.shape
    levels = courant.shape[1] // lat_rows
    field_count = channels // levels
    hidden = weight_in.shape[1]
    devices = lax.axis_size("gx")
    capacity = max(2, 2 * lat_rows // devices)
    window = min(lat_rows, -(-(capacity + ALIGN - 1) // ALIGN) * ALIGN)

    packed = pack_bands(weight_mid, bias_mid, weight_out, bias_out)
    packed = lax.all_gather(packed, "gx", axis=0, tiled=True)

    band_index = jnp.arange(devices, dtype=jnp.int32)
    first_lat = jnp.sum((strip_table[None, :] < band_index[:, None]).astype(jnp.int32), 1)
    end_lat = jnp.sum((strip_table[None, :] <= band_index[:, None]).astype(jnp.int32), 1)
    start = jnp.minimum((first_lat // ALIGN) * ALIGN, lat_rows - window).astype(jnp.int32)

    columns_bf = fields.astype(jnp.bfloat16)
    west_col = passed_along(columns_bf[-1:], "gx", 1)
    east_col = passed_along(columns_bf[:1], "gx", -1)
    padded = jnp.concatenate([west_col, columns_bf, east_col], 0)
    padded = jnp.pad(padded, ((0, 0), (1, 1), (0, 0)))
    kernel = weight_in.reshape(3, 3, channels, hidden)
    summed = lax.conv_general_dilated(
        padded[None],
        kernel,
        (1, 1),
        "VALID",
        dimension_numbers=("NHWC", "HWIO", "NHWC"),
        preferred_element_type=jnp.float32,
    )[0]
    summed = summed + bias_in
    hidden_one = jax.nn.silu(summed).astype(jnp.bfloat16)

    speeds = widened(courant.reshape(lon_dev, lat_rows, levels), field_count)
    switch_one = widened(switches[0].reshape(lon_dev, lat_rows, levels).astype(jnp.float32), field_count)
    switch_two = widened(switches[1].reshape(lon_dev, lat_rows, levels).astype(jnp.float32), field_count)
    ahead_col = east_col.astype(jnp.float32)
    section_one = fields - flux_change(fields, ahead_col, speeds, switch_one)
    ahead_two = passed_along(section_one[:1].astype(jnp.bfloat16), "gx", -1).astype(jnp.float32)
    section_two = section_one - flux_change(section_one, ahead_two, speeds, switch_two)
    moved = 0.5 * fields + 0.5 * section_two
    return band_networks(hidden_one, moved, packed, first_lat, end_lat, start, window)


def solution(mesh):
    return jax.shard_map(
        on_device,
        mesh=mesh,
        in_specs=(
            P(("group", "gx"), None, None),
            P(("group", "gx"), None),
            P(None, ("group", "gx"), None),
            P("group"),
            P(),
            P(),
            P("gx", None, None),
            P("gx", None),
            P("gx", None, None),
            P("gx", None),
        ),
        out_specs=P(("group", "gx"), None, None),
        check_vma=False,
    )
```

```python
import jax
import jax.numpy as jnp
from jax import lax
from jax.experimental import pallas as pl
from jax.experimental.pallas import tpu as pltpu
from jax.sharding import PartitionSpec as P

BIAS_ROWS = 16
ALIGN = 16
RESIDENT_BYTES = 8 * 1024 * 1024


def passed_along(array, axis, by):
    length = lax.axis_size(axis)
    return lax.ppermute(array, axis, [(i, (i + by) % length) for i in range(length)])


def split_three(values):
    high = values.astype(jnp.bfloat16)
    rest = values - high.astype(jnp.float32)
    middle = rest.astype(jnp.bfloat16)
    low = (rest - middle.astype(jnp.float32)).astype(jnp.bfloat16)
    return [high, middle, low]


def pack_layer(weight, bias):
    rows = jnp.stack(split_three(bias[0]), 0)
    rows = jnp.pad(rows, ((0, BIAS_ROWS - rows.shape[0]), (0, 0)))
    return jnp.concatenate([weight[0], rows], 0)[None]


def split_rows(bias_ref, first, row):
    lanes = bias_ref.shape[-1]
    values = jnp.broadcast_to(bias_ref[...].astype(jnp.float32), (BIAS_ROWS, lanes))
    high = values.astype(jnp.bfloat16).astype(jnp.float32)
    rest = values - high
    middle = rest.astype(jnp.bfloat16).astype(jnp.float32)
    low = (rest - middle).astype(jnp.bfloat16).astype(jnp.float32)
    return jnp.where(row == first, high, jnp.where(row == first + 1, middle, jnp.where(row == first + 2, low, 0.0)))


def pack_kernel(wm_hbm, bm_ref, wo_hbm, bo_ref, out_hbm, rows_ref, sem):
    inner = wm_hbm.shape[1]
    lanes = wm_hbm.shape[2]
    copies = [
        pltpu.make_async_copy(wm_hbm.at[0], out_hbm.at[0, pl.ds(0, inner)], sem.at[0]),
        pltpu.make_async_copy(wo_hbm.at[0], out_hbm.at[0, pl.ds(inner, inner)], sem.at[1]),
    ]
    for copy in copies:
        copy.start()
    row = lax.broadcasted_iota(jnp.int32, (BIAS_ROWS, lanes), 0)
    rows = split_rows(bm_ref, 0, row) + split_rows(bo_ref, 3, row)
    rows_ref[...] = rows.astype(jnp.bfloat16)
    last = pltpu.make_async_copy(rows_ref, out_hbm.at[0, pl.ds(2 * inner, BIAS_ROWS)], sem.at[2])
    last.start()
    for copy in copies:
        copy.wait()
    last.wait()


def pack_bands(weight_mid, bias_mid, weight_out, bias_out):
    inner, lanes = weight_mid.shape[1:]
    hbm = pl.BlockSpec(memory_space=pl.ANY)
    vmem = pl.BlockSpec(memory_space=pltpu.VMEM)
    return pl.pallas_call(
        pack_kernel,
        in_specs=[hbm, vmem, hbm, vmem],
        out_specs=hbm,
        out_shape=jax.ShapeDtypeStruct((1, 2 * inner + BIAS_ROWS, lanes), weight_mid.dtype),
        scratch_shapes=[pltpu.VMEM((BIAS_ROWS, lanes), weight_mid.dtype), pltpu.SemaphoreType.DMA((3,))],
    )(weight_mid, bias_mid, weight_out, bias_out)


def face_flux(left_vals, right_vals, speeds, switch_now):
    damping = switch_now * speeds * speeds + (1.0 - switch_now) * jnp.abs(speeds)
    return 0.5 * speeds * (left_vals + right_vals) - 0.5 * damping * (right_vals - left_vals)


def flux_change(values, right_col, speeds, switch_now):
    right_vals = jnp.concatenate([values[1:], right_col], 0)
    edge_flux = face_flux(values, right_vals, speeds, switch_now)
    left_flux = passed_along(edge_flux[-1:].astype(jnp.bfloat16), "gx", 1).astype(jnp.float32)
    return edge_flux - jnp.concatenate([left_flux, edge_flux[:-1]], 0)


def make_band_kernel(window, depth, resident):
    def kernel(lo_ref, hi_ref, start_ref, h1_ref, moved_ref, w_hbm, out_ref, *scratch):
        bands = w_hbm.shape[0]
        lon = h1_ref.shape[0]
        inner = h1_ref.shape[-1]
        if resident:
            wbuf = w_hbm
        else:
            wbuf, sem = scratch

            def fetch(band, slot):
                return pltpu.make_async_copy(w_hbm.at[band], wbuf.at[slot], sem.at[slot])

            for band in range(depth):
                fetch(band, band).start()

        def body(band, carry):
            if resident:
                slot = band
            else:
                slot = band % depth
                fetch(band, slot).wait()
            start = pl.multiple_of(start_ref[band], ALIGN)
            block = jnp.concatenate([h1_ref[l, pl.ds(start, window), :] for l in range(lon)], 0)
            weight_mid = wbuf[slot, 0:inner, :]
            weight_out = wbuf[slot, inner : 2 * inner, :]
            parts = wbuf[slot, 2 * inner : 2 * inner + 8, :].astype(jnp.float32)
            bias_mid = (parts[0:1] + parts[1:2]) + parts[2:3]
            bias_out = (parts[3:4] + parts[4:5]) + parts[5:6]
            middle = jnp.dot(block, weight_mid, preferred_element_type=jnp.float32) + bias_mid
            hidden_two = (middle / (1.0 + jnp.exp(-middle))).astype(jnp.bfloat16)
            result = jnp.dot(hidden_two, weight_out, preferred_element_type=jnp.float32) + bias_out
            result = result.astype(jnp.bfloat16).astype(jnp.float32)

            if not resident:

                @pl.when(band + depth < bands)
                def _():
                    fetch(band + depth, slot).start()

            lats = start + lax.broadcasted_iota(jnp.int32, (window, 1), 0)
            mask = jnp.logical_and(lats >= lo_ref[band], lats < hi_ref[band])
            for l in range(lon):
                current = out_ref[l, pl.ds(start, window), :]
                piece = result[l * window : (l + 1) * window]
                fresh = moved_ref[l, pl.ds(start, window), :] + piece
                out_ref[l, pl.ds(start, window), :] = jnp.where(mask, fresh, current)
            return carry

        lax.fori_loop(0, bands, body, 0, unroll=True if bands <= 16 else 4)

    return kernel


def band_networks(hidden_one, moved, packed, lo, hi, start, window):
    bands = packed.shape[0]
    depth = min(bands, 16)
    resident = packed.size * packed.dtype.itemsize <= RESIDENT_BYTES
    smem = pl.BlockSpec(memory_space=pltpu.SMEM)
    vmem = pl.BlockSpec(memory_space=pltpu.VMEM)
    if resident:
        weights_spec, scratch = vmem, []
    else:
        weights_spec = pl.BlockSpec(memory_space=pl.ANY)
        scratch = [
            pltpu.VMEM((depth,) + packed.shape[1:], packed.dtype),
            pltpu.SemaphoreType.DMA((depth,)),
        ]
    return pl.pallas_call(
        make_band_kernel(window, depth, resident),
        in_specs=[smem, smem, smem, vmem, vmem, weights_spec],
        out_specs=vmem,
        out_shape=jax.ShapeDtypeStruct(moved.shape, moved.dtype),
        scratch_shapes=scratch,
    )(lo, hi, start, hidden_one, moved, packed)


def widened(values, field_count):
    lon, rows, levels = values.shape
    return jnp.broadcast_to(values[:, :, None, :], (lon, rows, field_count, levels)).reshape(
        lon, rows, field_count * levels
    )


def on_device(
    fields,
    courant,
    switches,
    strip_table,
    weight_in,
    bias_in,
    weight_mid,
    bias_mid,
    weight_out,
    bias_out,
):
    lon_dev, lat_rows, channels = fields.shape
    levels = courant.shape[1] // lat_rows
    field_count = channels // levels
    hidden = weight_in.shape[1]
    devices = lax.axis_size("gx")
    capacity = max(2, 2 * lat_rows // devices)
    window = min(lat_rows, -(-(capacity + ALIGN - 1) // ALIGN) * ALIGN)

    packed = pack_bands(weight_mid, bias_mid, weight_out, bias_out)
    packed = lax.all_gather(packed, "gx", axis=0, tiled=True)

    band_index = jnp.arange(devices, dtype=jnp.int32)
    first_lat = jnp.sum((strip_table[None, :] < band_index[:, None]).astype(jnp.int32), 1)
    end_lat = jnp.sum((strip_table[None, :] <= band_index[:, None]).astype(jnp.int32), 1)
    start = jnp.minimum((first_lat // ALIGN) * ALIGN, lat_rows - window).astype(jnp.int32)

    columns_bf = fields.astype(jnp.bfloat16)
    west_col = passed_along(columns_bf[-1:], "gx", 1)
    east_col = passed_along(columns_bf[:1], "gx", -1)
    padded = jnp.concatenate([west_col, columns_bf, east_col], 0)
    padded = jnp.pad(padded, ((0, 0), (1, 1), (0, 0)))
    kernel = weight_in.reshape(3, 3, channels, hidden)
    summed = lax.conv_general_dilated(
        padded[None],
        kernel,
        (1, 1),
        "VALID",
        dimension_numbers=("NHWC", "HWIO", "NHWC"),
        preferred_element_type=jnp.float32,
    )[0]
    summed = summed + bias_in
    hidden_one = jax.nn.silu(summed).astype(jnp.bfloat16)

    speeds = widened(courant.reshape(lon_dev, lat_rows, levels), field_count)
    switch_one = widened(switches[0].reshape(lon_dev, lat_rows, levels).astype(jnp.float32), field_count)
    switch_two = widened(switches[1].reshape(lon_dev, lat_rows, levels).astype(jnp.float32), field_count)
    ahead_col = east_col.astype(jnp.float32)
    section_one = fields - flux_change(fields, ahead_col, speeds, switch_one)
    ahead_two = passed_along(section_one[:1].astype(jnp.bfloat16), "gx", -1).astype(jnp.float32)
    section_two = section_one - flux_change(section_one, ahead_two, speeds, switch_two)
    moved = 0.5 * fields + 0.5 * section_two
    return band_networks(hidden_one, moved, packed, first_lat, end_lat, start, window)


def solution(mesh):
    return jax.shard_map(
        on_device,
        mesh=mesh,
        in_specs=(
            P(("group", "gx"), None, None),
            P(("group", "gx"), None),
            P(None, ("group", "gx"), None),
            P("group"),
            P(),
            P(),
            P("gx", None, None),
            P("gx", None),
            P("gx", None, None),
            P("gx", None),
        ),
        out_specs=P(("group", "gx"), None, None),
        check_vma=False,
    )
```

```python
import jax
import jax.numpy as jnp
from jax import lax
from jax.experimental import pallas as pl
from jax.experimental.pallas import tpu as pltpu
from jax.sharding import PartitionSpec as P

BIAS_ROWS = 16
ALIGN = 16
RESIDENT_BYTES = 8 * 1024 * 1024


def passed_along(array, axis, by):
    length = lax.axis_size(axis)
    return lax.ppermute(array, axis, [(i, (i + by) % length) for i in range(length)])


def split_three(values):
    high = values.astype(jnp.bfloat16)
    rest = values - high.astype(jnp.float32)
    middle = rest.astype(jnp.bfloat16)
    low = (rest - middle.astype(jnp.float32)).astype(jnp.bfloat16)
    return [high, middle, low]


def pack_layer(weight, bias):
    rows = jnp.stack(split_three(bias[0]), 0)
    rows = jnp.pad(rows, ((0, BIAS_ROWS - rows.shape[0]), (0, 0)))
    return jnp.concatenate([weight[0], rows], 0)[None]


def split_rows(bias_ref, first, row):
    lanes = bias_ref.shape[-1]
    values = jnp.broadcast_to(bias_ref[...].astype(jnp.float32), (BIAS_ROWS, lanes))
    high = values.astype(jnp.bfloat16).astype(jnp.float32)
    rest = values - high
    middle = rest.astype(jnp.bfloat16).astype(jnp.float32)
    low = (rest - middle).astype(jnp.bfloat16).astype(jnp.float32)
    return jnp.where(row == first, high, jnp.where(row == first + 1, middle, jnp.where(row == first + 2, low, 0.0)))


def pack_kernel(bm_ref, bo_ref, out_ref):
    lanes = bm_ref.shape[-1]
    row = lax.broadcasted_iota(jnp.int32, (BIAS_ROWS, lanes), 0)
    rows = split_rows(bm_ref, 0, row) + split_rows(bo_ref, 3, row)
    out_ref[...] = rows.astype(jnp.bfloat16)


def pack_bands(weight_mid, bias_mid, weight_out, bias_out):
    lanes = weight_mid.shape[-1]
    rows = pl.pallas_call(
        pack_kernel,
        out_shape=jax.ShapeDtypeStruct((BIAS_ROWS, lanes), weight_mid.dtype),
    )(bias_mid, bias_out)
    return jnp.concatenate([weight_mid[0], weight_out[0], rows], 0)[None]


def face_flux(left_vals, right_vals, speeds, switch_now):
    damping = switch_now * speeds * speeds + (1.0 - switch_now) * jnp.abs(speeds)
    return 0.5 * speeds * (left_vals + right_vals) - 0.5 * damping * (right_vals - left_vals)


def flux_change(values, right_col, speeds, switch_now):
    right_vals = jnp.concatenate([values[1:], right_col], 0)
    edge_flux = face_flux(values, right_vals, speeds, switch_now)
    left_flux = passed_along(edge_flux[-1:].astype(jnp.bfloat16), "gx", 1).astype(jnp.float32)
    return edge_flux - jnp.concatenate([left_flux, edge_flux[:-1]], 0)


def make_band_kernel(window, depth, resident):
    def kernel(lo_ref, hi_ref, start_ref, h1_ref, moved_ref, w_hbm, out_ref, *scratch):
        out_ref[...] = moved_ref[...]
        bands = w_hbm.shape[0]
        lon = h1_ref.shape[0]
        inner = h1_ref.shape[-1]
        if resident:
            wbuf = w_hbm
        else:
            wbuf, sem = scratch

            def fetch(band, slot):
                return pltpu.make_async_copy(w_hbm.at[band], wbuf.at[slot], sem.at[slot])

            for band in range(depth):
                fetch(band, band).start()

        def body(band, carry):
            if resident:
                slot = band
            else:
                slot = band % depth
                fetch(band, slot).wait()
            start = pl.multiple_of(start_ref[band], ALIGN)
            block = jnp.concatenate([h1_ref[l, pl.ds(start, window), :] for l in range(lon)], 0)
            weight_mid = wbuf[slot, 0:inner, :]
            weight_out = wbuf[slot, inner : 2 * inner, :]
            parts = wbuf[slot, 2 * inner : 2 * inner + 8, :].astype(jnp.float32)
            bias_mid = (parts[0:1] + parts[1:2]) + parts[2:3]
            bias_out = (parts[3:4] + parts[4:5]) + parts[5:6]
            middle = jnp.dot(block, weight_mid, preferred_element_type=jnp.float32) + bias_mid
            hidden_two = (middle / (1.0 + jnp.exp(-middle))).astype(jnp.bfloat16)
            result = jnp.dot(hidden_two, weight_out, preferred_element_type=jnp.float32) + bias_out
            result = result.astype(jnp.bfloat16).astype(jnp.float32)

            if not resident:

                @pl.when(band + depth < bands)
                def _():
                    fetch(band + depth, slot).start()

            lats = start + lax.broadcasted_iota(jnp.int32, (window, 1), 0)
            mask = jnp.logical_and(lats >= lo_ref[band], lats < hi_ref[band])
            for l in range(lon):
                current = out_ref[l, pl.ds(start, window), :]
                piece = result[l * window : (l + 1) * window]
                out_ref[l, pl.ds(start, window), :] = jnp.where(mask, current + piece, current)
            return carry

        lax.fori_loop(0, bands, body, 0, unroll=True if bands <= 16 else 4)

    return kernel


def band_networks(hidden_one, moved, packed, lo, hi, start, window):
    bands = packed.shape[0]
    depth = min(bands, 16)
    resident = packed.size * packed.dtype.itemsize <= RESIDENT_BYTES
    smem = pl.BlockSpec(memory_space=pltpu.SMEM)
    vmem = pl.BlockSpec(memory_space=pltpu.VMEM)
    if resident:
        weights_spec, scratch = vmem, []
    else:
        weights_spec = pl.BlockSpec(memory_space=pl.ANY)
        scratch = [
            pltpu.VMEM((depth,) + packed.shape[1:], packed.dtype),
            pltpu.SemaphoreType.DMA((depth,)),
        ]
    return pl.pallas_call(
        make_band_kernel(window, depth, resident),
        in_specs=[smem, smem, smem, vmem, vmem, weights_spec],
        out_specs=vmem,
        out_shape=jax.ShapeDtypeStruct(moved.shape, moved.dtype),
        scratch_shapes=scratch,
    )(lo, hi, start, hidden_one, moved, packed)


def widened(values, field_count):
    lon, rows, levels = values.shape
    return jnp.broadcast_to(values[:, :, None, :], (lon, rows, field_count, levels)).reshape(
        lon, rows, field_count * levels
    )


def on_device(
    fields,
    courant,
    switches,
    strip_table,
    weight_in,
    bias_in,
    weight_mid,
    bias_mid,
    weight_out,
    bias_out,
):
    lon_dev, lat_rows, channels = fields.shape
    levels = courant.shape[1] // lat_rows
    field_count = channels // levels
    hidden = weight_in.shape[1]
    devices = lax.axis_size("gx")
    capacity = max(2, 2 * lat_rows // devices)
    window = min(lat_rows, -(-(capacity + ALIGN - 1) // ALIGN) * ALIGN)

    packed = pack_bands(weight_mid, bias_mid, weight_out, bias_out)
    packed = lax.all_gather(packed, "gx", axis=0, tiled=True)

    band_index = jnp.arange(devices, dtype=jnp.int32)
    first_lat = jnp.sum((strip_table[None, :] < band_index[:, None]).astype(jnp.int32), 1)
    end_lat = jnp.sum((strip_table[None, :] <= band_index[:, None]).astype(jnp.int32), 1)
    start = jnp.minimum((first_lat // ALIGN) * ALIGN, lat_rows - window).astype(jnp.int32)

    columns_bf = fields.astype(jnp.bfloat16)
    west_col = passed_along(columns_bf[-1:], "gx", 1)
    east_col = passed_along(columns_bf[:1], "gx", -1)
    padded = jnp.concatenate([west_col, columns_bf, east_col], 0)
    padded = jnp.pad(padded, ((0, 0), (1, 1), (0, 0)))
    kernel = weight_in.reshape(3, 3, channels, hidden)
    summed = lax.conv_general_dilated(
        padded[None],
        kernel,
        (1, 1),
        "VALID",
        dimension_numbers=("NHWC", "HWIO", "NHWC"),
        preferred_element_type=jnp.float32,
    )[0]
    summed = summed + bias_in
    hidden_one = jax.nn.silu(summed).astype(jnp.bfloat16)

    speeds = widened(courant.reshape(lon_dev, lat_rows, levels), field_count)
    switch_one = widened(switches[0].reshape(lon_dev, lat_rows, levels).astype(jnp.float32), field_count)
    switch_two = widened(switches[1].reshape(lon_dev, lat_rows, levels).astype(jnp.float32), field_count)
    ahead_col = east_col.astype(jnp.float32)
    section_one = fields - flux_change(fields, ahead_col, speeds, switch_one)
    ahead_two = passed_along(section_one[:1].astype(jnp.bfloat16), "gx", -1).astype(jnp.float32)
    section_two = section_one - flux_change(section_one, ahead_two, speeds, switch_two)
    moved = 0.5 * fields + 0.5 * section_two
    return band_networks(hidden_one, moved, packed, first_lat, end_lat, start, window)


def solution(mesh):
    return jax.shard_map(
        on_device,
        mesh=mesh,
        in_specs=(
            P(("group", "gx"), None, None),
            P(("group", "gx"), None),
            P(None, ("group", "gx"), None),
            P("group"),
            P(),
            P(),
            P("gx", None, None),
            P("gx", None),
            P("gx", None, None),
            P("gx", None),
        ),
        out_specs=P(("group", "gx"), None, None),
        check_vma=False,
    )
```
